256 devices in a mesh: sec: 2 (over y_hi), gx: 32 (over z, y_lo, core), gy: 4 (over x).
Axes of the slice: x: 4, y: 4 (y_hi: 2, y_lo: 2; y = y_hi * 2 + y_lo), z: 8, core: 2. Of those that a mesh axis runs over, the one named last changes fastest.
Arguments:
- model_state: float32 [2, 3, 32, 512, 2048], P('sec', None, None, 'gx', 'gy'), may hold values from -6 to 6
- wave_speed: float32 [2, 512, 2048], P('sec', 'gx', 'gy'), may hold values from 0.05 to 0.45
- wet_mask: int32 [2, 512, 2048], P('sec', 'gx', 'gy'), may hold values 0 or 1
- vertical: float32 [2, 32, 32], P('sec'), may hold values from -1 to 1
- surface_temp: float32 [2, 512, 2048], P('sec', 'gx', 'gy'), may hold values from -6 to 6
- flux_coef: float32 [8, 4], replicated, may hold values from -3 to 3
- heat_gain: float32 [8], replicated, may hold values from -2.5 to 2.5
- pair_tile: int32 [32, 4, 64, 1], P('gx', 'gy'), may hold values from 0 to 31; in each aligned block of 64 rows (0 to 63, 64 to 127, ..., all dimensions but the last counted through in order) at most 4 rows name the same one
- pair_source: int32 [32, 4, 64], P('gx', 'gy'), may hold values from 0 to 31
- pair_target: int32 [32, 4, 64], P('gx', 'gy'), may hold values from 0 to 63
- intersection_weights: bfloat16 [32, 4, 64, 256, 128], P('gx', 'gy'), may hold values from -0.375 to 0.375
Outputs:
- final_state: float32 [2, 3, 32, 512, 2048], P('sec', None, None, 'gx', 'gy')
- surface_temps: float32 [2, 512, 2048], P('sec', 'gx', 'gy')
The draws below stay inside these ranges and needn't reach their ends.
Inputs may be any that keep to these rules, and one draw needn't show every extreme that they name: `pair_tile`: the destination lies in the source tile's column along gy; at most 4 pairs of one atmosphere tile name one ocean tile, and in some tile exactly 4 do.
All inputs are finite; a program needn't handle non-finite values. No bound on the sum of `wet_mask` on one device may be relied on, other than what follows from the above.
Results may differ from the reference program's by a relative error of at most 0.0033.
Values may be sent and summed in bfloat16 or wider, within the bound.
No kernel may reach another device: no remote copies, remote signals or barrier semaphores. Data moves between devices by JAX's collectives and lax.ppermute only.
A program may use at most 64 MiB of HBM per device.

```python
import math
import jax
import jax.numpy as jnp
import numpy as np
from jax import lax

LEV = 32
SUBSTEPS = 2
AX = 16
AY = 512
F = 8
RI = 256
RO = 128
KBA = 32
KBO = 64
P_SIZE = 64
CAP = 4
NX = 512
NY = 2048
N_GX = 32
N_GY = 4


def plant(drawn, key, least, high):
    longest = drawn.shape.index(max(drawn.shape))
    spots = []
    for shift in (0, 1):
        where = [jax.random.randint(jax.random.fold_in(key, axis), (), 0, length) for axis, length in enumerate(drawn.shape)]
        where[longest] = (where[longest] + shift) % drawn.shape[longest]
        spots.append(tuple(where))
    return drawn.at[spots[0]].set(least).at[spots[1]].set(high)


def steps_of(own_key, dims, shards, low, largest):
    gain, own = 1.0, jax.random.fold_in(own_key, 6)
    for axis_at, blocks in shards:
        heights = jnp.exp(jax.random.uniform(jax.random.fold_in(own, axis_at), (blocks,), jnp.float32, low / len(shards), largest / len(shards)))
        gain = gain * jnp.repeat(heights, dims[axis_at] // blocks).reshape([-1 if axis == axis_at else 1 for axis in range(len(dims))])
    return gain


def assign_block(stream_key, own, number, rows, amount, top, reach, skew):
    order = jax.random.permutation(stream_key, amount)
    heavy_load, common = portions_of(amount, rows * top, reach, skew, True), portions_of(amount, rows * top, reach, skew, False)
    places = jnp.arange(amount)

    def named(lengths, turn):
        used = int((lengths > 0).sum())
        fixed = max(1, used // 4)
        shifted = fixed + (places - fixed + turn * (used - fixed)) % max(1, amount - fixed)
        return jnp.zeros((amount,), jnp.int32).at[order[jnp.where(places < fixed, places, shifted)]].set(jnp.asarray(lengths, jnp.int32))

    lengths = jnp.where(number % 4 == 0, named(heavy_load, number // 4), named(common, number - number // 4 - 1))
    mixed = jax.random.permutation(jax.random.fold_in(own, 3), amount)
    donor, taker = mixed[0:amount // 2 * 2:2], mixed[1:amount // 2 * 2:2]
    room = jnp.minimum(lengths[donor] - 1, reach - lengths[taker]) // 2
    room = jnp.where((donor == order[0]) | (taker == order[0]) | (lengths[taker] == 0), 0, jnp.maximum(room, 0))
    shifted = jax.random.randint(jax.random.fold_in(own, 4), (amount // 2,), 0, 1 << 20) % (room + 1)
    lengths = lengths.at[donor].add(-shifted).at[taker].add(shifted)
    items = jnp.searchsorted(jnp.cumsum(lengths), jnp.arange(rows * top), side="right").astype(jnp.int32)
    listing = items.reshape(top, rows).T
    listing = listing[jax.random.permutation(jax.random.fold_in(own, 1), rows)]
    turn = jax.random.randint(jax.random.fold_in(own, 2), (rows, 1), 0, top)
    return jnp.take_along_axis(listing, (jnp.arange(top)[None, :] + turn) % top, axis=1)


def portions_of(number_of, total, reach, slope, full):
    loads = [(1 << 20) // math.isqrt(grade ** slope) + 1 for grade in range(1, number_of + 1)]
    largest = reach if full else min(reach, max(-(-total // number_of), total * loads[0] // sum(loads)))
    least = 1 if total - largest >= number_of - 1 else 0
    holding, spare = [largest] + [least] * (number_of - 1), total - largest - least * (number_of - 1)
    while spare > 0:
        candidates = [i for i in range(1, number_of) if holding[i] < largest] or [i for i in range(1, number_of) if holding[i] < reach]
        pool, left = sum([loads[i] for i in candidates]), spare
        for i in candidates:
            extra = min(reach - holding[i], max(1, left * loads[i] // pool), spare)
            holding[i] = holding[i] + extra
            spare = spare - extra
    return np.array(holding)


def noise(key, dims, width, bound, cuts=(), kind=jnp.bfloat16):
    result = width * jax.random.normal(key, dims, jnp.float32)
    if cuts:
        result = result * steps_of(key, dims, cuts, -0.22, 0.18)
    return jnp.clip(result, -bound, bound).astype(kind)


def setup_inputs(seed: int = 0) -> dict:
    key_of = jax.random.split(jax.random.key(seed), 12)
    model_state = noise(key_of[0], (2, 3, LEV, NX, NY), 1.0, 6.0, ((0, 2), (3, 32), (4, 4)), jnp.float32)
    wave_speed = jnp.clip(0.05 + 0.39999999 * jax.random.uniform(key_of[1], (2, NX, NY), jnp.float32) ** steps_of(key_of[1], (2, NX, NY), ((0, 2), (1, 32), (2, 4)), -0.2, 0.2), 0.05, 0.45)
    wet_mask = plant((jax.random.randint(key_of[2], (2, NX, NY), 0, 8) < 7).astype(jnp.int32), jax.random.fold_in(key_of[2], 1), 0, 1)
    vertical = noise(key_of[3], (2, LEV, LEV), LEV ** -0.5, 1.0, ((0, 2),), jnp.float32)
    surface_temp = noise(key_of[4], (2, NX, NY), 1.0, 6.0, ((0, 2), (1, 32), (2, 4)), jnp.float32)
    flux_coef = noise(key_of[5], (F, 4), 0.6, 3.0, (), jnp.float32)
    heat_gain = noise(key_of[6], (F,), 0.5, 2.5, (), jnp.float32)
    pair_tile_keys = jax.random.split(jax.random.fold_in(key_of[7], 1), N_GX * N_GY * P_SIZE // P_SIZE)
    pair_tile_turns = jax.random.permutation(jax.random.fold_in(key_of[7], 3), N_GX * N_GY * P_SIZE // P_SIZE)
    pair_tile = jax.vmap(lambda own, number: assign_block(jax.random.fold_in(key_of[7], 2), own, number, P_SIZE, N_GX, 1, CAP, 1))(pair_tile_keys, pair_tile_turns).reshape((N_GX, N_GY, P_SIZE, 1))
    pair_source = plant(jax.random.randint(key_of[8], (N_GX, N_GY, P_SIZE), 0, KBA), jax.random.fold_in(key_of[8], 1), 0, KBA - 1).astype(jnp.int32)
    pair_target = plant(jax.random.randint(key_of[9], (N_GX, N_GY, P_SIZE), 0, KBO), jax.random.fold_in(key_of[9], 1), 0, KBO - 1).astype(jnp.int32)
    intersection_weights = noise(key_of[10], (N_GX, N_GY, P_SIZE, RI, RO), RI ** -0.5, 0.375, ((0, 32), (1, 4)))
    return {"model_state": model_state, "wave_speed": wave_speed, "wet_mask": wet_mask, "vertical": vertical, "surface_temp": surface_temp, "flux_coef": flux_coef, "heat_gain": heat_gain, "pair_tile": pair_tile, "pair_source": pair_source, "pair_target": pair_target, "intersection_weights": intersection_weights}


HIGHEST_PRECISION = lax.Precision.HIGHEST


def eastern(values):
    return jnp.pad(values, ((0, 0), (0, 1), (0, 0)))[:, 1:, :]


def western(values):
    return jnp.pad(values, ((0, 0), (1, 0), (0, 0)))[:, :-1, :]


def northern(values):
    return jnp.pad(values, ((0, 0), (0, 0), (0, 1)))[:, :, 1:]


def southern(values):
    return jnp.pad(values, ((0, 0), (0, 0), (1, 0)))[:, :, :-1]


def vertical_mix(matrix, right_side):
    return right_side + jnp.einsum("lm,mxy->lxy", matrix, right_side, precision=HIGHEST_PRECISION)


def make_tiles(values):
    return values.reshape(N_GX, AX, N_GY, AY).transpose(0, 2, 1, 3).reshape(N_GX, N_GY, AX * AY)


def join_tiles(values):
    return values.reshape(N_GX, N_GY, AX, AY).transpose(0, 2, 1, 3).reshape(N_GX * AX, N_GY * AY)


def reference(model_state, wave_speed, wet_mask, vertical, surface_temp, flux_coef, heat_gain, pair_tile, pair_source, pair_target, intersection_weights):
    finals = []
    for section in range(2):
        pressure = model_state[section, 0]
        eastward = model_state[section, 1]
        northward = model_state[section, 2]
        sound_speed = wave_speed[section]
        wetness = wet_mask[section].astype(jnp.float32)
        matrix = vertical[section]
        for substep in range(SUBSTEPS):
            divergence = (eastern(eastward) - western(eastward)) + (northern(northward) - southern(northward))
            pressure = vertical_mix(matrix, pressure - sound_speed * divergence)
            eastward = wetness * (eastward - 0.5 * (eastern(pressure) - western(pressure)))
            northward = wetness * (northward - 0.5 * (northern(pressure) - southern(pressure)))
        finals.append(jnp.stack([pressure, eastward, northward]))
    final_state = jnp.stack(finals)

    drivers = jnp.stack([make_tiles(model_state[0, 0, 0]), make_tiles(model_state[0, 1, 0]), make_tiles(model_state[0, 2, 0]), make_tiles(surface_temp[0])], axis=2)
    fluxes = jnp.tanh(jnp.einsum("fk,abkc->abfc", flux_coef, drivers, precision=HIGHEST_PRECISION)).astype(jnp.bfloat16)
    blocks = fluxes.reshape(N_GX, N_GY, F, KBA, RI).transpose(0, 1, 3, 2, 4)
    across = jnp.arange(N_GX, dtype=jnp.int32)[:, None, None]
    within = jnp.arange(N_GY, dtype=jnp.int32)[None, :, None]
    picked = blocks[across, within, pair_source]
    weights_wide = intersection_weights.astype(jnp.float32)
    regridded = jnp.einsum("abpfi,abpio->abpfo", picked.astype(jnp.float32), weights_wide, precision=HIGHEST_PRECISION).astype(jnp.bfloat16)
    target_tile = pair_tile[..., 0]
    ocean_blocks = jnp.zeros((N_GX, N_GY, KBO, F, RO), jnp.float32).at[target_tile, within, pair_target].add(regridded.astype(jnp.float32))
    ocean_flux = ocean_blocks.transpose(0, 1, 3, 2, 4).reshape(N_GX, N_GY, F, KBO * RO)
    heating = jnp.einsum("f,abfc->abc", heat_gain, ocean_flux, precision=HIGHEST_PRECISION)
    ocean_temp = make_tiles(surface_temp[1]) + make_tiles(wet_mask[1].astype(jnp.float32)) * heating
    returned = ocean_temp.astype(jnp.bfloat16).reshape(N_GX, N_GY, KBO, RO)[target_tile, within, pair_target]
    pieces = jnp.einsum("abpio,abpo->abpi", weights_wide, returned.astype(jnp.float32), precision=HIGHEST_PRECISION)
    atmos_blocks = jnp.zeros((N_GX, N_GY, KBA, RI), jnp.float32).at[across, within, pair_source].add(pieces)
    surface_temps = jnp.stack([join_tiles(atmos_blocks.reshape(N_GX, N_GY, AX * AY)), join_tiles(ocean_temp)])
    return final_state, surface_temps
```

```python
import jax
import jax.numpy as jnp
from jax import lax
from jax.sharding import PartitionSpec as P

SUBSTEPS = 2


HIGHEST_PRECISION = lax.Precision.HIGHEST


def neighbours(head, tail, axis):
    count = lax.axis_size(axis)
    lo = lax.ppermute(tail, axis, [(i, i + 1) for i in range(count - 1)])
    hi = lax.ppermute(head, axis, [(i + 1, i) for i in range(count - 1)])
    return lo, hi


def vertical_mix(matrix, right_side):
    return right_side + jnp.einsum("lm,mxy->lxy", matrix, right_side, precision=HIGHEST_PRECISION)


def stencil(pressure, eastward, northward, sound_speed, wetness, matrix):
    wet3 = wetness[None]
    lo_x, hi_x = neighbours(
        jnp.concatenate([eastward[:, :1], wet3[:, :1]], axis=0),
        jnp.concatenate([eastward[:, -1:], wet3[:, -1:]], axis=0),
        "gx",
    )
    lo_y, hi_y = neighbours(
        jnp.concatenate([northward[:, :, :1], wet3[:, :, :1]], axis=0),
        jnp.concatenate([northward[:, :, -1:], wet3[:, :, -1:]], axis=0),
        "gy",
    )
    levels = eastward.shape[0]
    u_ext = jnp.concatenate([lo_x[:levels], eastward, hi_x[:levels]], axis=1)
    wet_x = jnp.concatenate([lo_x[levels:], wet3, hi_x[levels:]], axis=1)
    v_ext = jnp.concatenate([lo_y[:levels], northward, hi_y[:levels]], axis=2)
    wet_y = jnp.concatenate([lo_y[levels:], wet3, hi_y[levels:]], axis=2)

    divergence = (u_ext[:, 2:] - u_ext[:, :-2]) + (v_ext[:, :, 2:] - v_ext[:, :, :-2])
    p1 = vertical_mix(matrix, pressure - sound_speed * divergence)

    lo2x, hi2x = neighbours(p1[:, :2], p1[:, -2:], "gx")
    lo2y, hi2y = neighbours(p1[:, :, :2], p1[:, :, -2:], "gy")
    p1_x = jnp.concatenate([lo2x, p1, hi2x], axis=1)
    p1_y = jnp.concatenate([lo2y, p1, hi2y], axis=2)
    u1_ext = wet_x * (u_ext - 0.5 * (p1_x[:, 2:] - p1_x[:, :-2]))
    v1_ext = wet_y * (v_ext - 0.5 * (p1_y[:, :, 2:] - p1_y[:, :, :-2]))

    divergence = (u1_ext[:, 2:] - u1_ext[:, :-2]) + (v1_ext[:, :, 2:] - v1_ext[:, :, :-2])
    p2 = vertical_mix(matrix, p1 - sound_speed * divergence)

    lo3x, hi3x = neighbours(p2[:, :1], p2[:, -1:], "gx")
    lo3y, hi3y = neighbours(p2[:, :, :1], p2[:, :, -1:], "gy")
    p2_x = jnp.concatenate([lo3x, p2, hi3x], axis=1)
    p2_y = jnp.concatenate([lo3y, p2, hi3y], axis=2)
    u1 = u1_ext[:, 1:-1]
    v1 = v1_ext[:, :, 1:-1]
    u2 = wetness * (u1 - 0.5 * (p2_x[:, 2:] - p2_x[:, :-2]))
    v2 = wetness * (v1 - 0.5 * (p2_y[:, :, 2:] - p2_y[:, :, :-2]))
    return p2, u2, v2


def local(
    model_state,
    wave_speed,
    wet_mask,
    vertical,
    surface_temp,
    flux_coef,
    heat_gain,
    pair_tile,
    pair_source,
    pair_target,
    intersection_weights,
):
    pressure = model_state[0, 0]
    eastward = model_state[0, 1]
    northward = model_state[0, 2]
    sound_speed = wave_speed[0]
    wetness = wet_mask[0].astype(jnp.float32)
    matrix = vertical[0]
    assert SUBSTEPS == 2
    p2, u2, v2 = stencil(pressure, eastward, northward, sound_speed, wetness, matrix)
    final_state = jnp.stack([p2, u2, v2])[None]

    weights = intersection_weights[0, 0]
    pair_count, in_width, out_width = weights.shape
    tile_count = lax.axis_size("gx")
    grid_shape = surface_temp.shape[1:]
    cell_count = grid_shape[0] * grid_shape[1]
    in_blocks = cell_count // in_width
    out_blocks = cell_count // out_width
    sources = pair_source[0, 0]
    targets = pair_target[0, 0]
    target_tile = pair_tile[0, 0, :, 0]
    is_atmos = lax.axis_index("sec") == 0
    me = lax.axis_index("gx")

    own_st = surface_temp[0].reshape(cell_count)
    own_wet = wetness.reshape(cell_count)
    drivers = jnp.stack(
        [model_state[0, 0, 0].reshape(cell_count), model_state[0, 1, 0].reshape(cell_count),
         model_state[0, 2, 0].reshape(cell_count), own_st]
    )
    zeros = jnp.zeros_like(own_st)
    sent = jnp.where(is_atmos, drivers, jnp.stack([own_st, own_wet, zeros, zeros]))
    got = lax.ppermute(sent, "sec", [(0, 1), (1, 0)])
    atmos_drivers = jnp.where(is_atmos, drivers, got)
    ocean_st = jnp.where(is_atmos, got[0], own_st)
    ocean_wet = jnp.where(is_atmos, got[1], own_wet)

    pad = jnp.zeros((out_width - pair_count,), jnp.float32)
    table = jnp.concatenate(
        [
            ocean_st.reshape(out_blocks, out_width),
            ocean_wet.reshape(out_blocks, out_width),
            jnp.concatenate([target_tile.astype(jnp.float32), pad])[None],
            jnp.concatenate([targets.astype(jnp.float32), pad])[None],
        ]
    )
    tables = lax.all_gather(table, "gx")
    st_blocks = tables[:, :out_blocks].reshape(tile_count * out_blocks, out_width)
    wet_blocks = tables[:, out_blocks:2 * out_blocks].reshape(tile_count * out_blocks, out_width)
    all_tiles = tables[:, 2 * out_blocks, :pair_count].reshape(tile_count * pair_count).astype(jnp.int32)
    all_targets = tables[:, 2 * out_blocks + 1, :pair_count].reshape(tile_count * pair_count).astype(jnp.int32)

    fluxes = jnp.tanh(jnp.dot(flux_coef, atmos_drivers, precision=HIGHEST_PRECISION)).astype(jnp.bfloat16)
    flux_count = fluxes.shape[0]
    blocks = fluxes.reshape(flux_count, in_blocks, in_width)
    picked = jnp.take(blocks, sources, axis=1)
    regridded = jnp.einsum(
        "fpi,pio->pfo", picked, weights, preferred_element_type=jnp.float32
    ).astype(jnp.bfloat16)
    heat = jnp.einsum(
        "f,pfo->po", heat_gain, regridded.astype(jnp.float32), precision=HIGHEST_PRECISION
    )
    heats = lax.all_gather(heat, "gx").reshape(tile_count * pair_count, out_width)

    own_match = (all_tiles[None, :] == me) & (all_targets[None, :] == jnp.arange(out_blocks)[:, None])
    heating = jnp.dot(own_match.astype(jnp.float32), heats, precision=HIGHEST_PRECISION)
    ocean_temp = own_st + own_wet * heating.reshape(cell_count)

    pair_match = (all_tiles[None, :] == target_tile[:, None]) & (all_targets[None, :] == targets[:, None])
    pair_heating = jnp.dot(pair_match.astype(jnp.float32), heats, precision=HIGHEST_PRECISION)
    rows = target_tile * out_blocks + targets
    pair_temp = jnp.take(st_blocks, rows, axis=0) + jnp.take(wet_blocks, rows, axis=0) * pair_heating
    returned = pair_temp.astype(jnp.bfloat16)
    pieces = jnp.einsum("pio,po->pi", weights, returned, preferred_element_type=jnp.float32)
    owning = (jnp.arange(in_blocks)[:, None] == sources[None, :]).astype(jnp.float32)
    atmos_temp = jnp.dot(owning, pieces, precision=HIGHEST_PRECISION)

    surface_temps = jnp.where(is_atmos, atmos_temp.reshape(grid_shape), ocean_temp.reshape(grid_shape))[None]
    return (final_state, surface_temps)


def solution(mesh):
    return jax.shard_map(
        local,
        mesh=mesh,
        in_specs=(
            P("sec", None, None, "gx", "gy"),
            P("sec", "gx", "gy"),
            P("sec", "gx", "gy"),
            P("sec", None, None),
            P("sec", "gx", "gy"),
            P(),
            P(),
            P("gx", "gy", None, None),
            P("gx", "gy", None),
            P("gx", "gy", None),
            P("gx", "gy", None, None, None),
        ),
        out_specs=(P("sec", None, None, "gx", "gy"), P("sec", "gx", "gy")),
        check_vma=False,
    )
```

```python
import jax
import jax.numpy as jnp
from jax import lax
from jax.sharding import PartitionSpec as P

SUBSTEPS = 2


HIGHEST_PRECISION = lax.Precision.HIGHEST


def neighbours(head, tail, axis):
    count = lax.axis_size(axis)
    lo = lax.ppermute(tail, axis, [(i, i + 1) for i in range(count - 1)])
    hi = lax.ppermute(head, axis, [(i + 1, i) for i in range(count - 1)])
    return lo, hi


def vertical_mix(matrix, right_side):
    return right_side + jnp.einsum("lm,mxy->lxy", matrix, right_side, precision=HIGHEST_PRECISION)


def stencil(pressure, eastward, northward, sound_speed, wetness, matrix):
    wet3 = wetness[None]
    lo_x, hi_x = neighbours(
        jnp.concatenate([eastward[:, :1], wet3[:, :1]], axis=0),
        jnp.concatenate([eastward[:, -1:], wet3[:, -1:]], axis=0),
        "gx",
    )
    lo_y, hi_y = neighbours(
        jnp.concatenate([northward[:, :, :1], wet3[:, :, :1]], axis=0),
        jnp.concatenate([northward[:, :, -1:], wet3[:, :, -1:]], axis=0),
        "gy",
    )
    levels = eastward.shape[0]
    u_ext = jnp.concatenate([lo_x[:levels], eastward, hi_x[:levels]], axis=1)
    wet_x = jnp.concatenate([lo_x[levels:], wet3, hi_x[levels:]], axis=1)
    v_ext = jnp.concatenate([lo_y[:levels], northward, hi_y[:levels]], axis=2)
    wet_y = jnp.concatenate([lo_y[levels:], wet3, hi_y[levels:]], axis=2)

    divergence = (u_ext[:, 2:] - u_ext[:, :-2]) + (v_ext[:, :, 2:] - v_ext[:, :, :-2])
    p1 = vertical_mix(matrix, pressure - sound_speed * divergence)

    lo2x, hi2x = neighbours(p1[:, :2], p1[:, -2:], "gx")
    lo2y, hi2y = neighbours(p1[:, :, :2], p1[:, :, -2:], "gy")
    p1_x = jnp.concatenate([lo2x, p1, hi2x], axis=1)
    p1_y = jnp.concatenate([lo2y, p1, hi2y], axis=2)
    u1_ext = wet_x * (u_ext - 0.5 * (p1_x[:, 2:] - p1_x[:, :-2]))
    v1_ext = wet_y * (v_ext - 0.5 * (p1_y[:, :, 2:] - p1_y[:, :, :-2]))

    divergence = (u1_ext[:, 2:] - u1_ext[:, :-2]) + (v1_ext[:, :, 2:] - v1_ext[:, :, :-2])
    p2 = vertical_mix(matrix, p1 - sound_speed * divergence)

    lo3x, hi3x = neighbours(p2[:, :1], p2[:, -1:], "gx")
    lo3y, hi3y = neighbours(p2[:, :, :1], p2[:, :, -1:], "gy")
    p2_x = jnp.concatenate([lo3x, p2, hi3x], axis=1)
    p2_y = jnp.concatenate([lo3y, p2, hi3y], axis=2)
    u1 = u1_ext[:, 1:-1]
    v1 = v1_ext[:, :, 1:-1]
    u2 = wetness * (u1 - 0.5 * (p2_x[:, 2:] - p2_x[:, :-2]))
    v2 = wetness * (v1 - 0.5 * (p2_y[:, :, 2:] - p2_y[:, :, :-2]))
    return p2, u2, v2


def local(
    model_state,
    wave_speed,
    wet_mask,
    vertical,
    surface_temp,
    flux_coef,
    heat_gain,
    pair_tile,
    pair_source,
    pair_target,
    intersection_weights,
):
    pressure = model_state[0, 0]
    eastward = model_state[0, 1]
    northward = model_state[0, 2]
    sound_speed = wave_speed[0]
    wetness = wet_mask[0].astype(jnp.float32)
    matrix = vertical[0]
    assert SUBSTEPS == 2
    p2, u2, v2 = stencil(pressure, eastward, northward, sound_speed, wetness, matrix)
    final_state = jnp.stack([p2, u2, v2])[None]

    weights = intersection_weights[0, 0]
    pair_count, in_width, out_width = weights.shape
    tile_count = lax.axis_size("gx")
    grid_shape = surface_temp.shape[1:]
    cell_count = grid_shape[0] * grid_shape[1]
    in_blocks = cell_count // in_width
    out_blocks = cell_count // out_width
    sources = pair_source[0, 0]
    targets = pair_target[0, 0]
    target_tile = pair_tile[0, 0, :, 0]
    is_atmos = lax.axis_index("sec") == 0

    own_st = surface_temp[0].reshape(cell_count)
    own_wet = wetness.reshape(cell_count)
    drivers = jnp.stack(
        [model_state[0, 0, 0].reshape(cell_count), model_state[0, 1, 0].reshape(cell_count),
         model_state[0, 2, 0].reshape(cell_count), own_st]
    )
    zeros = jnp.zeros_like(own_st)
    sent = jnp.where(is_atmos, drivers, jnp.stack([own_st, own_wet, zeros, zeros]))
    got = lax.ppermute(sent, "sec", [(0, 1), (1, 0)])
    atmos_drivers = jnp.where(is_atmos, drivers, got)
    ocean_st = jnp.where(is_atmos, got[0], own_st)
    ocean_wet = jnp.where(is_atmos, got[1], own_wet)

    fluxes = jnp.tanh(jnp.dot(flux_coef, atmos_drivers, precision=HIGHEST_PRECISION)).astype(jnp.bfloat16)
    flux_count = fluxes.shape[0]
    blocks = fluxes.reshape(flux_count, in_blocks, in_width)
    picked = jnp.take(blocks, sources, axis=1)
    regridded = jnp.einsum(
        "fpi,pio->pfo", picked, weights, preferred_element_type=jnp.float32
    ).astype(jnp.bfloat16)
    heat = jnp.einsum(
        "f,pfo->po", heat_gain, regridded.astype(jnp.float32), precision=HIGHEST_PRECISION
    )

    capacity = max(2, 2 * pair_count // tile_count)
    slot_count = tile_count * capacity
    positions = jnp.arange(pair_count)
    same_tile = target_tile[None, :] == target_tile[:, None]
    is_before = positions[None, :] < positions[:, None]
    earlier = jnp.sum(same_tile & is_before, axis=1)
    slot_of = target_tile * capacity + earlier
    placing = jnp.arange(slot_count)[:, None] == slot_of[None, :]
    outgoing = jnp.dot(placing.astype(jnp.float32), heat, precision=HIGHEST_PRECISION)
    offsets = jnp.sum(jnp.where(placing, targets[None, :] + 1, 0), axis=1) - 1
    offset_row = jnp.zeros((tile_count, 1, out_width), jnp.float32).at[:, 0, :capacity].set(
        offsets.reshape(tile_count, capacity).astype(jnp.float32)
    )
    packet = jnp.concatenate([outgoing.reshape(tile_count, capacity, out_width), offset_row], axis=1)
    arrived = lax.all_to_all(packet, "gx", split_axis=0, concat_axis=0, tiled=True)
    arrived_at = arrived[:, capacity, :capacity].reshape(slot_count).astype(jnp.int32)
    landing = jnp.arange(out_blocks)[:, None] == arrived_at[None, :]
    heating = jnp.dot(
        landing.astype(jnp.float32),
        arrived[:, :capacity].reshape(slot_count, out_width),
        precision=HIGHEST_PRECISION,
    )
    ocean_temp = ocean_st + ocean_wet * heating.reshape(cell_count)

    returning = jnp.dot(
        landing.T.astype(jnp.bfloat16),
        ocean_temp.astype(jnp.bfloat16).reshape(out_blocks, out_width),
        preferred_element_type=jnp.float32,
    ).astype(jnp.bfloat16)
    delivered = lax.all_to_all(
        returning.reshape(tile_count, capacity, out_width), "gx", split_axis=0, concat_axis=0, tiled=True
    )
    per_pair = jnp.dot(
        placing.T.astype(jnp.bfloat16),
        delivered.reshape(slot_count, out_width),
        preferred_element_type=jnp.float32,
    ).astype(jnp.bfloat16)
    pieces = jnp.einsum("pio,po->pi", weights, per_pair, preferred_element_type=jnp.float32)
    owning = (jnp.arange(in_blocks)[:, None] == sources[None, :]).astype(jnp.float32)
    atmos_temp = jnp.dot(owning, pieces, precision=HIGHEST_PRECISION)

    surface_temps = jnp.where(is_atmos, atmos_temp.reshape(grid_shape), ocean_temp.reshape(grid_shape))[None]
    return (final_state, surface_temps)


def solution(mesh):
    return jax.shard_map(
        local,
        mesh=mesh,
        in_specs=(
            P("sec", None, None, "gx", "gy"),
            P("sec", "gx", "gy"),
            P("sec", "gx", "gy"),
            P("sec", None, None),
            P("sec", "gx", "gy"),
            P(),
            P(),
            P("gx", "gy", None, None),
            P("gx", "gy", None),
            P("gx", "gy", None),
            P("gx", "gy", None, None, None),
        ),
        out_specs=(P("sec", None, None, "gx", "gy"), P("sec", "gx", "gy")),
        check_vma=False,
    )
```

```python
import jax
import jax.numpy as jnp
from jax import lax
from jax.sharding import PartitionSpec as P

SUBSTEPS = 2


HIGHEST_PRECISION = lax.Precision.HIGHEST


def neighbours(head, tail, axis):
    count = lax.axis_size(axis)
    lo = lax.ppermute(tail, axis, [(i, i + 1) for i in range(count - 1)])
    hi = lax.ppermute(head, axis, [(i + 1, i) for i in range(count - 1)])
    return lo, hi


def vertical_mix(matrix, right_side):
    return right_side + jnp.sum(matrix[:, :, None, None] * right_side[None], axis=1)


def stencil(pressure, eastward, northward, sound_speed, wetness, matrix):
    wet3 = wetness[None]
    lo_x, hi_x = neighbours(
        jnp.concatenate([eastward[:, :1], wet3[:, :1]], axis=0),
        jnp.concatenate([eastward[:, -1:], wet3[:, -1:]], axis=0),
        "gx",
    )
    lo_y, hi_y = neighbours(
        jnp.concatenate([northward[:, :, :1], wet3[:, :, :1]], axis=0),
        jnp.concatenate([northward[:, :, -1:], wet3[:, :, -1:]], axis=0),
        "gy",
    )
    levels = eastward.shape[0]
    u_ext = jnp.concatenate([lo_x[:levels], eastward, hi_x[:levels]], axis=1)
    wet_x = jnp.concatenate([lo_x[levels:], wet3, hi_x[levels:]], axis=1)
    v_ext = jnp.concatenate([lo_y[:levels], northward, hi_y[:levels]], axis=2)
    wet_y = jnp.concatenate([lo_y[levels:], wet3, hi_y[levels:]], axis=2)

    divergence = (u_ext[:, 2:] - u_ext[:, :-2]) + (v_ext[:, :, 2:] - v_ext[:, :, :-2])
    p1 = vertical_mix(matrix, pressure - sound_speed * divergence)

    lo2x, hi2x = neighbours(p1[:, :2], p1[:, -2:], "gx")
    lo2y, hi2y = neighbours(p1[:, :, :2], p1[:, :, -2:], "gy")
    p1_x = jnp.concatenate([lo2x, p1, hi2x], axis=1)
    p1_y = jnp.concatenate([lo2y, p1, hi2y], axis=2)
    u1_ext = wet_x * (u_ext - 0.5 * (p1_x[:, 2:] - p1_x[:, :-2]))
    v1_ext = wet_y * (v_ext - 0.5 * (p1_y[:, :, 2:] - p1_y[:, :, :-2]))

    divergence = (u1_ext[:, 2:] - u1_ext[:, :-2]) + (v1_ext[:, :, 2:] - v1_ext[:, :, :-2])
    p2 = vertical_mix(matrix, p1 - sound_speed * divergence)

    lo3x, hi3x = neighbours(p2[:, :1], p2[:, -1:], "gx")
    lo3y, hi3y = neighbours(p2[:, :, :1], p2[:, :, -1:], "gy")
    p2_x = jnp.concatenate([lo3x, p2, hi3x], axis=1)
    p2_y = jnp.concatenate([lo3y, p2, hi3y], axis=2)
    u1 = u1_ext[:, 1:-1]
    v1 = v1_ext[:, :, 1:-1]
    u2 = wetness * (u1 - 0.5 * (p2_x[:, 2:] - p2_x[:, :-2]))
    v2 = wetness * (v1 - 0.5 * (p2_y[:, :, 2:] - p2_y[:, :, :-2]))
    return p2, u2, v2


def local(
    model_state,
    wave_speed,
    wet_mask,
    vertical,
    surface_temp,
    flux_coef,
    heat_gain,
    pair_tile,
    pair_source,
    pair_target,
    intersection_weights,
):
    pressure = model_state[0, 0]
    eastward = model_state[0, 1]
    northward = model_state[0, 2]
    sound_speed = wave_speed[0]
    wetness = wet_mask[0].astype(jnp.float32)
    matrix = vertical[0]
    assert SUBSTEPS == 2
    p2, u2, v2 = stencil(pressure, eastward, northward, sound_speed, wetness, matrix)
    final_state = jnp.stack([p2, u2, v2])[None]

    weights = intersection_weights[0, 0]
    pair_count, in_width, out_width = weights.shape
    tile_count = lax.axis_size("gx")
    grid_shape = surface_temp.shape[1:]
    cell_count = grid_shape[0] * grid_shape[1]
    in_blocks = cell_count // in_width
    out_blocks = cell_count // out_width
    sources = pair_source[0, 0]
    targets = pair_target[0, 0]
    target_tile = pair_tile[0, 0, :, 0]
    is_atmos = lax.axis_index("sec") == 0

    own_st = surface_temp[0].reshape(cell_count)
    own_wet = wetness.reshape(cell_count)
    drivers = jnp.stack(
        [model_state[0, 0, 0].reshape(cell_count), model_state[0, 1, 0].reshape(cell_count),
         model_state[0, 2, 0].reshape(cell_count), own_st]
    )
    zeros = jnp.zeros_like(own_st)
    sent = jnp.where(is_atmos, drivers, jnp.stack([own_st, own_wet, zeros, zeros]))
    got = lax.ppermute(sent, "sec", [(0, 1), (1, 0)])
    atmos_drivers = jnp.where(is_atmos, drivers, got)
    ocean_st = jnp.where(is_atmos, got[0], own_st)
    ocean_wet = jnp.where(is_atmos, got[1], own_wet)

    fluxes = jnp.tanh(jnp.dot(flux_coef, atmos_drivers, precision=HIGHEST_PRECISION)).astype(jnp.bfloat16)
    flux_count = fluxes.shape[0]
    blocks = fluxes.reshape(flux_count, in_blocks, in_width)
    picked = jnp.take(blocks, sources, axis=1)
    regridded = jnp.einsum(
        "fpi,pio->pfo", picked, weights, preferred_element_type=jnp.float32
    ).astype(jnp.bfloat16)
    heat = jnp.einsum(
        "f,pfo->po", heat_gain, regridded.astype(jnp.float32), precision=HIGHEST_PRECISION
    )

    capacity = max(2, 2 * pair_count // tile_count)
    slot_count = tile_count * capacity
    positions = jnp.arange(pair_count)
    same_tile = target_tile[None, :] == target_tile[:, None]
    is_before = positions[None, :] < positions[:, None]
    earlier = jnp.sum(same_tile & is_before, axis=1)
    slot_of = target_tile * capacity + earlier
    placing = jnp.arange(slot_count)[:, None] == slot_of[None, :]
    outgoing = jnp.dot(placing.astype(jnp.float32), heat, precision=HIGHEST_PRECISION)
    offsets = jnp.sum(jnp.where(placing, targets[None, :] + 1, 0), axis=1) - 1
    offset_row = jnp.zeros((tile_count, 1, out_width), jnp.float32).at[:, 0, :capacity].set(
        offsets.reshape(tile_count, capacity).astype(jnp.float32)
    )
    packet = jnp.concatenate([outgoing.reshape(tile_count, capacity, out_width), offset_row], axis=1)
    arrived = lax.all_to_all(packet, "gx", split_axis=0, concat_axis=0, tiled=True)
    arrived_at = arrived[:, capacity, :capacity].reshape(slot_count).astype(jnp.int32)
    landing = jnp.arange(out_blocks)[:, None] == arrived_at[None, :]
    heating = jnp.dot(
        landing.astype(jnp.float32),
        arrived[:, :capacity].reshape(slot_count, out_width),
        precision=HIGHEST_PRECISION,
    )
    ocean_temp = ocean_st + ocean_wet * heating.reshape(cell_count)

    returning = jnp.dot(
        landing.T.astype(jnp.bfloat16),
        ocean_temp.astype(jnp.bfloat16).reshape(out_blocks, out_width),
        preferred_element_type=jnp.float32,
    ).astype(jnp.bfloat16)
    delivered = lax.all_to_all(
        returning.reshape(tile_count, capacity, out_width), "gx", split_axis=0, concat_axis=0, tiled=True
    )
    per_pair = jnp.dot(
        placing.T.astype(jnp.bfloat16),
        delivered.reshape(slot_count, out_width),
        preferred_element_type=jnp.float32,
    ).astype(jnp.bfloat16)
    pieces = jnp.einsum("pio,po->pi", weights, per_pair, preferred_element_type=jnp.float32)
    owning = (jnp.arange(in_blocks)[:, None] == sources[None, :]).astype(jnp.float32)
    atmos_temp = jnp.dot(owning, pieces, precision=HIGHEST_PRECISION)

    surface_temps = jnp.where(is_atmos, atmos_temp.reshape(grid_shape), ocean_temp.reshape(grid_shape))[None]
    return (final_state, surface_temps)


def solution(mesh):
    return jax.shard_map(
        local,
        mesh=mesh,
        in_specs=(
            P("sec", None, None, "gx", "gy"),
            P("sec", "gx", "gy"),
            P("sec", "gx", "gy"),
            P("sec", None, None),
            P("sec", "gx", "gy"),
            P(),
            P(),
            P("gx", "gy", None, None),
            P("gx", "gy", None),
            P("gx", "gy", None),
            P("gx", "gy", None, None, None),
        ),
        out_specs=(P("sec", None, None, "gx", "gy"), P("sec", "gx", "gy")),
        check_vma=False,
    )
```

```python
import jax
import jax.numpy as jnp
from jax import lax
from jax.sharding import PartitionSpec as P

SUBSTEPS = 2


HIGHEST_PRECISION = lax.Precision.HIGHEST


def neighbours(head, tail, axis):
    count = lax.axis_size(axis)
    lo = lax.ppermute(tail, axis, [(i, i + 1) for i in range(count - 1)])
    hi = lax.ppermute(head, axis, [(i + 1, i) for i in range(count - 1)])
    return lo, hi


def staged_all_to_all(values, inner=4):
    count = lax.axis_size("gx")
    outer = count // inner
    near = [[o * inner + i for i in range(inner)] for o in range(outer)]
    far = [[o * inner + i for o in range(outer)] for i in range(inner)]
    rest = values.shape[1:]
    values = values.reshape(outer, inner, *rest)
    values = lax.all_to_all(values, "gx", 1, 1, axis_index_groups=near, tiled=True)
    values = lax.all_to_all(values, "gx", 0, 0, axis_index_groups=far, tiled=True)
    return values.reshape(count, *rest)


def vertical_mix(matrix, right_side):
    return right_side + jnp.einsum("lm,mxy->lxy", matrix, right_side, precision=HIGHEST_PRECISION)


def stencil(pressure, eastward, northward, sound_speed, wetness, matrix):
    wet3 = wetness[None]
    lo_x, hi_x = neighbours(
        jnp.concatenate([eastward[:, :1], wet3[:, :1]], axis=0),
        jnp.concatenate([eastward[:, -1:], wet3[:, -1:]], axis=0),
        "gx",
    )
    lo_y, hi_y = neighbours(
        jnp.concatenate([northward[:, :, :1], wet3[:, :, :1]], axis=0),
        jnp.concatenate([northward[:, :, -1:], wet3[:, :, -1:]], axis=0),
        "gy",
    )
    levels = eastward.shape[0]
    u_ext = jnp.concatenate([lo_x[:levels], eastward, hi_x[:levels]], axis=1)
    wet_x = jnp.concatenate([lo_x[levels:], wet3, hi_x[levels:]], axis=1)
    v_ext = jnp.concatenate([lo_y[:levels], northward, hi_y[:levels]], axis=2)
    wet_y = jnp.concatenate([lo_y[levels:], wet3, hi_y[levels:]], axis=2)

    divergence = (u_ext[:, 2:] - u_ext[:, :-2]) + (v_ext[:, :, 2:] - v_ext[:, :, :-2])
    p1 = vertical_mix(matrix, pressure - sound_speed * divergence)

    lo2x, hi2x = neighbours(p1[:, :2], p1[:, -2:], "gx")
    lo2y, hi2y = neighbours(p1[:, :, :2], p1[:, :, -2:], "gy")
    p1_x = jnp.concatenate([lo2x, p1, hi2x], axis=1)
    p1_y = jnp.concatenate([lo2y, p1, hi2y], axis=2)
    u1_ext = wet_x * (u_ext - 0.5 * (p1_x[:, 2:] - p1_x[:, :-2]))
    v1_ext = wet_y * (v_ext - 0.5 * (p1_y[:, :, 2:] - p1_y[:, :, :-2]))

    divergence = (u1_ext[:, 2:] - u1_ext[:, :-2]) + (v1_ext[:, :, 2:] - v1_ext[:, :, :-2])
    p2 = vertical_mix(matrix, p1 - sound_speed * divergence)

    lo3x, hi3x = neighbours(p2[:, :1], p2[:, -1:], "gx")
    lo3y, hi3y = neighbours(p2[:, :, :1], p2[:, :, -1:], "gy")
    p2_x = jnp.concatenate([lo3x, p2, hi3x], axis=1)
    p2_y = jnp.concatenate([lo3y, p2, hi3y], axis=2)
    u1 = u1_ext[:, 1:-1]
    v1 = v1_ext[:, :, 1:-1]
    u2 = wetness * (u1 - 0.5 * (p2_x[:, 2:] - p2_x[:, :-2]))
    v2 = wetness * (v1 - 0.5 * (p2_y[:, :, 2:] - p2_y[:, :, :-2]))
    return p2, u2, v2


def local(
    model_state,
    wave_speed,
    wet_mask,
    vertical,
    surface_temp,
    flux_coef,
    heat_gain,
    pair_tile,
    pair_source,
    pair_target,
    intersection_weights,
):
    pressure = model_state[0, 0]
    eastward = model_state[0, 1]
    northward = model_state[0, 2]
    sound_speed = wave_speed[0]
    wetness = wet_mask[0].astype(jnp.float32)
    matrix = vertical[0]
    assert SUBSTEPS == 2
    p2, u2, v2 = stencil(pressure, eastward, northward, sound_speed, wetness, matrix)
    final_state = jnp.stack([p2, u2, v2])[None]

    weights = intersection_weights[0, 0]
    pair_count, in_width, out_width = weights.shape
    tile_count = lax.axis_size("gx")
    grid_shape = surface_temp.shape[1:]
    cell_count = grid_shape[0] * grid_shape[1]
    in_blocks = cell_count // in_width
    out_blocks = cell_count // out_width
    sources = pair_source[0, 0]
    targets = pair_target[0, 0]
    target_tile = pair_tile[0, 0, :, 0]
    is_atmos = lax.axis_index("sec") == 0

    own_st = surface_temp[0].reshape(cell_count)
    own_wet = wetness.reshape(cell_count)
    drivers = jnp.stack(
        [model_state[0, 0, 0].reshape(cell_count), model_state[0, 1, 0].reshape(cell_count),
         model_state[0, 2, 0].reshape(cell_count), own_st]
    )
    zeros = jnp.zeros_like(own_st)
    sent = jnp.where(is_atmos, drivers, jnp.stack([own_st, own_wet, zeros, zeros]))
    got = lax.ppermute(sent, "sec", [(0, 1), (1, 0)])
    atmos_drivers = jnp.where(is_atmos, drivers, got)
    ocean_st = jnp.where(is_atmos, got[0], own_st)
    ocean_wet = jnp.where(is_atmos, got[1], own_wet)

    fluxes = jnp.tanh(jnp.dot(flux_coef, atmos_drivers, precision=HIGHEST_PRECISION)).astype(jnp.bfloat16)
    flux_count = fluxes.shape[0]
    blocks = fluxes.reshape(flux_count, in_blocks, in_width)
    picked = jnp.take(blocks, sources, axis=1)
    regridded = jnp.einsum(
        "fpi,pio->pfo", picked, weights, preferred_element_type=jnp.float32
    ).astype(jnp.bfloat16)
    heat = jnp.einsum(
        "f,pfo->po", heat_gain, regridded.astype(jnp.float32), precision=HIGHEST_PRECISION
    )

    capacity = max(2, 2 * pair_count // tile_count)
    slot_count = tile_count * capacity
    positions = jnp.arange(pair_count)
    same_tile = target_tile[None, :] == target_tile[:, None]
    is_before = positions[None, :] < positions[:, None]
    earlier = jnp.sum(same_tile & is_before, axis=1)
    slot_of = target_tile * capacity + earlier
    placing = jnp.arange(slot_count)[:, None] == slot_of[None, :]
    outgoing = jnp.dot(placing.astype(jnp.float32), heat, precision=HIGHEST_PRECISION)
    offsets = jnp.sum(jnp.where(placing, targets[None, :] + 1, 0), axis=1) - 1
    offset_row = jnp.zeros((tile_count, 1, out_width), jnp.float32).at[:, 0, :capacity].set(
        offsets.reshape(tile_count, capacity).astype(jnp.float32)
    )
    packet = jnp.concatenate([outgoing.reshape(tile_count, capacity, out_width), offset_row], axis=1)
    arrived = staged_all_to_all(packet)
    arrived_at = arrived[:, capacity, :capacity].reshape(slot_count).astype(jnp.int32)
    landing = jnp.arange(out_blocks)[:, None] == arrived_at[None, :]
    heating = jnp.dot(
        landing.astype(jnp.float32),
        arrived[:, :capacity].reshape(slot_count, out_width),
        precision=HIGHEST_PRECISION,
    )
    ocean_temp = ocean_st + ocean_wet * heating.reshape(cell_count)

    returning = jnp.dot(
        landing.T.astype(jnp.bfloat16),
        ocean_temp.astype(jnp.bfloat16).reshape(out_blocks, out_width),
        preferred_element_type=jnp.float32,
    ).astype(jnp.bfloat16)
    delivered = staged_all_to_all(returning.reshape(tile_count, capacity, out_width))
    per_pair = jnp.dot(
        placing.T.astype(jnp.bfloat16),
        delivered.reshape(slot_count, out_width),
        preferred_element_type=jnp.float32,
    ).astype(jnp.bfloat16)
    pieces = jnp.einsum("pio,po->pi", weights, per_pair, preferred_element_type=jnp.float32)
    owning = (jnp.arange(in_blocks)[:, None] == sources[None, :]).astype(jnp.float32)
    atmos_temp = jnp.dot(owning, pieces, precision=HIGHEST_PRECISION)

    surface_temps = jnp.where(is_atmos, atmos_temp.reshape(grid_shape), ocean_temp.reshape(grid_shape))[None]
    return (final_state, surface_temps)


def solution(mesh):
    return jax.shard_map(
        local,
        mesh=mesh,
        in_specs=(
            P("sec", None, None, "gx", "gy"),
            P("sec", "gx", "gy"),
            P("sec", "gx", "gy"),
            P("sec", None, None),
            P("sec", "gx", "gy"),
            P(),
            P(),
            P("gx", "gy", None, None),
            P("gx", "gy", None),
            P("gx", "gy", None),
            P("gx", "gy", None, None, None),
        ),
        out_specs=(P("sec", None, None, "gx", "gy"), P("sec", "gx", "gy")),
        check_vma=False,
    )
```

```python
import jax
import jax.numpy as jnp
from jax import lax
from jax.sharding import PartitionSpec as P

SUBSTEPS = 2


HIGHEST_PRECISION = lax.Precision.HIGHEST


def neighbours(head, tail, axis):
    count = lax.axis_size(axis)
    lo = lax.ppermute(tail, axis, [(i, i + 1) for i in range(count - 1)])
    hi = lax.ppermute(head, axis, [(i + 1, i) for i in range(count - 1)])
    return lo, hi


def vertical_mix(matrix, right_side):
    return right_side + jnp.einsum("lm,mxy->lxy", matrix, right_side, precision=HIGHEST_PRECISION)


def stencil(pressure, eastward, northward, sound_speed, wetness, matrix):
    wet3 = wetness[None]
    lo_x, hi_x = neighbours(
        jnp.concatenate([eastward[:, :1], wet3[:, :1]], axis=0),
        jnp.concatenate([eastward[:, -1:], wet3[:, -1:]], axis=0),
        "gx",
    )
    lo_y, hi_y = neighbours(
        jnp.concatenate([northward[:, :, :1], wet3[:, :, :1]], axis=0),
        jnp.concatenate([northward[:, :, -1:], wet3[:, :, -1:]], axis=0),
        "gy",
    )
    levels = eastward.shape[0]
    u_ext = jnp.concatenate([lo_x[:levels], eastward, hi_x[:levels]], axis=1)
    wet_x = jnp.concatenate([lo_x[levels:], wet3, hi_x[levels:]], axis=1)
    v_ext = jnp.concatenate([lo_y[:levels], northward, hi_y[:levels]], axis=2)
    wet_y = jnp.concatenate([lo_y[levels:], wet3, hi_y[levels:]], axis=2)

    divergence = (u_ext[:, 2:] - u_ext[:, :-2]) + (v_ext[:, :, 2:] - v_ext[:, :, :-2])
    p1 = vertical_mix(matrix, pressure - sound_speed * divergence)

    lo2x, hi2x = neighbours(p1[:, :2], p1[:, -2:], "gx")
    lo2y, hi2y = neighbours(p1[:, :, :2], p1[:, :, -2:], "gy")
    p1_x = jnp.concatenate([lo2x, p1, hi2x], axis=1)
    p1_y = jnp.concatenate([lo2y, p1, hi2y], axis=2)
    u1_ext = wet_x * (u_ext - 0.5 * (p1_x[:, 2:] - p1_x[:, :-2]))
    v1_ext = wet_y * (v_ext - 0.5 * (p1_y[:, :, 2:] - p1_y[:, :, :-2]))

    divergence = (u1_ext[:, 2:] - u1_ext[:, :-2]) + (v1_ext[:, :, 2:] - v1_ext[:, :, :-2])
    p2 = vertical_mix(matrix, p1 - sound_speed * divergence)

    lo3x, hi3x = neighbours(p2[:, :1], p2[:, -1:], "gx")
    lo3y, hi3y = neighbours(p2[:, :, :1], p2[:, :, -1:], "gy")
    p2_x = jnp.concatenate([lo3x, p2, hi3x], axis=1)
    p2_y = jnp.concatenate([lo3y, p2, hi3y], axis=2)
    u1 = u1_ext[:, 1:-1]
    v1 = v1_ext[:, :, 1:-1]
    u2 = wetness * (u1 - 0.5 * (p2_x[:, 2:] - p2_x[:, :-2]))
    v2 = wetness * (v1 - 0.5 * (p2_y[:, :, 2:] - p2_y[:, :, :-2]))
    return p2, u2, v2


def coupling_head(model_state, wetness, surface_temp, flux_coef, heat_gain, sources, targets, target_tile, weights):
    pair_count, in_width, out_width = weights.shape
    grid_shape = surface_temp.shape[1:]
    cell_count = grid_shape[0] * grid_shape[1]
    in_blocks = cell_count // in_width
    out_blocks = cell_count // out_width
    is_atmos = lax.axis_index("sec") == 0

    own_st = surface_temp[0].reshape(cell_count)
    own_wet = wetness.reshape(cell_count)
    drivers = jnp.stack(
        [model_state[0, 0, 0].reshape(cell_count), model_state[0, 1, 0].reshape(cell_count),
         model_state[0, 2, 0].reshape(cell_count), own_st]
    )
    zeros = jnp.zeros_like(own_st)
    sent = jnp.where(is_atmos, drivers, jnp.stack([own_st, own_wet, zeros, zeros]))
    got = lax.ppermute(sent, "sec", [(0, 1), (1, 0)])
    atmos_drivers = jnp.where(is_atmos, drivers, got)
    ocean_st = jnp.where(is_atmos, got[0], own_st)
    ocean_wet = jnp.where(is_atmos, got[1], own_wet)

    fluxes = jnp.tanh(jnp.dot(flux_coef, atmos_drivers, precision=HIGHEST_PRECISION)).astype(jnp.bfloat16)
    flux_count = fluxes.shape[0]
    blocks = fluxes.reshape(flux_count, in_blocks, in_width)
    picked = jnp.take(blocks, sources, axis=1)
    regridded = jnp.einsum(
        "fpi,pio->pfo", picked, weights, preferred_element_type=jnp.float32
    ).astype(jnp.bfloat16)
    heat = jnp.einsum(
        "f,pfo->po", heat_gain, regridded.astype(jnp.float32), precision=HIGHEST_PRECISION
    )

    index_row = jnp.zeros((1, out_width), jnp.float32)
    index_row = index_row.at[0, :pair_count].set(target_tile.astype(jnp.float32))
    index_row = index_row.at[0, out_width - pair_count:].set(targets.astype(jnp.float32))
    return jnp.concatenate(
        [heat, ocean_st.reshape(out_blocks, out_width), ocean_wet.reshape(out_blocks, out_width), index_row]
    )


def coupling_tail(tables, surface_temp, wetness, sources, targets, target_tile, weights):
    tile_count, rows, out_width = tables.shape
    pair_count, in_width, _ = weights.shape
    grid_shape = surface_temp.shape[1:]
    cell_count = grid_shape[0] * grid_shape[1]
    in_blocks = cell_count // in_width
    out_blocks = cell_count // out_width
    me = lax.axis_index("gx")
    heats = tables[:, :pair_count].reshape(tile_count * pair_count, out_width)
    st_blocks = tables[:, pair_count:pair_count + out_blocks].reshape(tile_count * out_blocks, out_width)
    wet_blocks = tables[:, pair_count + out_blocks:pair_count + 2 * out_blocks].reshape(
        tile_count * out_blocks, out_width
    )
    index_rows = tables[:, pair_count + 2 * out_blocks]
    all_tiles = index_rows[:, :pair_count].reshape(tile_count * pair_count).astype(jnp.int32)
    all_targets = index_rows[:, out_width - pair_count:].reshape(tile_count * pair_count).astype(jnp.int32)

    own_match = (all_tiles[None, :] == me) & (all_targets[None, :] == jnp.arange(out_blocks)[:, None])
    heating = jnp.dot(own_match.astype(jnp.float32), heats, precision=HIGHEST_PRECISION)
    ocean_temp = surface_temp[0] + wetness * heating.reshape(grid_shape)

    pair_match = (all_tiles[None, :] == target_tile[:, None]) & (all_targets[None, :] == targets[:, None])
    pair_heating = jnp.dot(pair_match.astype(jnp.float32), heats, precision=HIGHEST_PRECISION)
    picks = target_tile * out_blocks + targets
    pair_temp = jnp.take(st_blocks, picks, axis=0) + jnp.take(wet_blocks, picks, axis=0) * pair_heating
    returned = pair_temp.astype(jnp.bfloat16)
    pieces = jnp.einsum("pio,po->pi", weights, returned, preferred_element_type=jnp.float32)
    owning = (jnp.arange(in_blocks)[:, None] == sources[None, :]).astype(jnp.float32)
    atmos_temp = jnp.dot(owning, pieces, precision=HIGHEST_PRECISION).reshape(grid_shape)
    is_atmos = lax.axis_index("sec") == 0
    return jnp.where(is_atmos, atmos_temp, ocean_temp)[None]


def local(
    model_state,
    wave_speed,
    wet_mask,
    vertical,
    surface_temp,
    flux_coef,
    heat_gain,
    pair_tile,
    pair_source,
    pair_target,
    intersection_weights,
):
    weights = intersection_weights[0, 0]
    sources = pair_source[0, 0]
    targets = pair_target[0, 0]
    target_tile = pair_tile[0, 0, :, 0]
    wetness = wet_mask[0].astype(jnp.float32)
    table = coupling_head(
        model_state, wetness, surface_temp, flux_coef, heat_gain, sources, targets, target_tile, weights
    )
    table, pressure = lax.optimization_barrier((table, model_state[0, 0]))
    tables = lax.all_gather(table, "gx")

    eastward = model_state[0, 1]
    northward = model_state[0, 2]
    sound_speed = wave_speed[0]
    matrix = vertical[0]
    assert SUBSTEPS == 2
    p2, u2, v2 = stencil(pressure, eastward, northward, sound_speed, wetness, matrix)
    final_state = jnp.stack([p2, u2, v2])[None]
    surface_temps = coupling_tail(tables, surface_temp, wetness, sources, targets, target_tile, weights)
    return (final_state, surface_temps)


def solution(mesh):
    return jax.shard_map(
        local,
        mesh=mesh,
        in_specs=(
            P("sec", None, None, "gx", "gy"),
            P("sec", "gx", "gy"),
            P("sec", "gx", "gy"),
            P("sec", None, None),
            P("sec", "gx", "gy"),
            P(),
            P(),
            P("gx", "gy", None, None),
            P("gx", "gy", None),
            P("gx", "gy", None),
            P("gx", "gy", None, None, None),
        ),
        out_specs=(P("sec", None, None, "gx", "gy"), P("sec", "gx", "gy")),
        check_vma=False,
    )
```

```python
import jax
import jax.numpy as jnp
from jax import lax
from jax.sharding import PartitionSpec as P

SUBSTEPS = 2


HIGHEST_PRECISION = lax.Precision.HIGHEST


def neighbours(head, tail, axis):
    count = lax.axis_size(axis)
    lo = lax.ppermute(tail, axis, [(i, i + 1) for i in range(count - 1)])
    hi = lax.ppermute(head, axis, [(i + 1, i) for i in range(count - 1)])
    return lo, hi


def vertical_mix(matrix, right_side):
    return right_side + jnp.einsum("lm,mxy->lxy", matrix, right_side, precision=HIGHEST_PRECISION)


def stencil(pressure, eastward, northward, sound_speed, wetness, matrix, stages):
    wet3 = wetness[None]
    lo_x, hi_x = neighbours(
        jnp.concatenate([eastward[:, :1], wet3[:, :1]], axis=0),
        jnp.concatenate([eastward[:, -1:], wet3[:, -1:]], axis=0),
        "gx",
    )
    lo_y, hi_y = neighbours(
        jnp.concatenate([northward[:, :, :1], wet3[:, :, :1]], axis=0),
        jnp.concatenate([northward[:, :, -1:], wet3[:, :, -1:]], axis=0),
        "gy",
    )
    lo_x, hi_x, lo_y, hi_y = stages[0]((lo_x, hi_x, lo_y, hi_y))
    levels = eastward.shape[0]
    u_ext = jnp.concatenate([lo_x[:levels], eastward, hi_x[:levels]], axis=1)
    wet_x = jnp.concatenate([lo_x[levels:], wet3, hi_x[levels:]], axis=1)
    v_ext = jnp.concatenate([lo_y[:levels], northward, hi_y[:levels]], axis=2)
    wet_y = jnp.concatenate([lo_y[levels:], wet3, hi_y[levels:]], axis=2)

    divergence = (u_ext[:, 2:] - u_ext[:, :-2]) + (v_ext[:, :, 2:] - v_ext[:, :, :-2])
    p1 = vertical_mix(matrix, pressure - sound_speed * divergence)

    lo2x, hi2x = neighbours(p1[:, :2], p1[:, -2:], "gx")
    lo2y, hi2y = neighbours(p1[:, :, :2], p1[:, :, -2:], "gy")
    lo2x, hi2x, lo2y, hi2y = stages[1]((lo2x, hi2x, lo2y, hi2y))
    p1_x = jnp.concatenate([lo2x, p1, hi2x], axis=1)
    p1_y = jnp.concatenate([lo2y, p1, hi2y], axis=2)
    u1_ext = wet_x * (u_ext - 0.5 * (p1_x[:, 2:] - p1_x[:, :-2]))
    v1_ext = wet_y * (v_ext - 0.5 * (p1_y[:, :, 2:] - p1_y[:, :, :-2]))

    divergence = (u1_ext[:, 2:] - u1_ext[:, :-2]) + (v1_ext[:, :, 2:] - v1_ext[:, :, :-2])
    p2 = vertical_mix(matrix, p1 - sound_speed * divergence)

    lo3x, hi3x = neighbours(p2[:, :1], p2[:, -1:], "gx")
    lo3y, hi3y = neighbours(p2[:, :, :1], p2[:, :, -1:], "gy")
    lo3x, hi3x, lo3y, hi3y = stages[2]((lo3x, hi3x, lo3y, hi3y))
    p2_x = jnp.concatenate([lo3x, p2, hi3x], axis=1)
    p2_y = jnp.concatenate([lo3y, p2, hi3y], axis=2)
    u1 = u1_ext[:, 1:-1]
    v1 = v1_ext[:, :, 1:-1]
    u2 = wetness * (u1 - 0.5 * (p2_x[:, 2:] - p2_x[:, :-2]))
    v2 = wetness * (v1 - 0.5 * (p2_y[:, :, 2:] - p2_y[:, :, :-2]))
    return p2, u2, v2


def local(
    model_state,
    wave_speed,
    wet_mask,
    vertical,
    surface_temp,
    flux_coef,
    heat_gain,
    pair_tile,
    pair_source,
    pair_target,
    intersection_weights,
):
    pressure = model_state[0, 0]
    eastward = model_state[0, 1]
    northward = model_state[0, 2]
    sound_speed = wave_speed[0]
    wetness = wet_mask[0].astype(jnp.float32)
    matrix = vertical[0]

    weights = intersection_weights[0, 0]
    pair_count, in_width, out_width = weights.shape
    tile_count = lax.axis_size("gx")
    grid_shape = surface_temp.shape[1:]
    cell_count = grid_shape[0] * grid_shape[1]
    in_blocks = cell_count // in_width
    out_blocks = cell_count // out_width
    sources = pair_source[0, 0]
    targets = pair_target[0, 0]
    target_tile = pair_tile[0, 0, :, 0]
    is_atmos = lax.axis_index("sec") == 0

    own_st = surface_temp[0].reshape(cell_count)
    own_wet = wetness.reshape(cell_count)
    drivers = jnp.stack(
        [model_state[0, 0, 0].reshape(cell_count), model_state[0, 1, 0].reshape(cell_count),
         model_state[0, 2, 0].reshape(cell_count), own_st]
    )
    zeros = jnp.zeros_like(own_st)
    sent = jnp.where(is_atmos, drivers, jnp.stack([own_st, own_wet, zeros, zeros]))
    got = lax.ppermute(sent, "sec", [(0, 1), (1, 0)])
    atmos_drivers = jnp.where(is_atmos, drivers, got)
    ocean_st = jnp.where(is_atmos, got[0], own_st)
    ocean_wet = jnp.where(is_atmos, got[1], own_wet)

    fluxes = jnp.tanh(jnp.dot(flux_coef, atmos_drivers, precision=HIGHEST_PRECISION)).astype(jnp.bfloat16)
    flux_count = fluxes.shape[0]
    blocks = fluxes.reshape(flux_count, in_blocks, in_width)
    picked = jnp.take(blocks, sources, axis=1)
    regridded = jnp.einsum(
        "fpi,pio->pfo", picked, weights, preferred_element_type=jnp.float32
    ).astype(jnp.bfloat16)
    heat = jnp.einsum(
        "f,pfo->po", heat_gain, regridded.astype(jnp.float32), precision=HIGHEST_PRECISION
    )

    capacity = max(2, 2 * pair_count // tile_count)
    slot_count = tile_count * capacity
    positions = jnp.arange(pair_count)
    same_tile = target_tile[None, :] == target_tile[:, None]
    is_before = positions[None, :] < positions[:, None]
    earlier = jnp.sum(same_tile & is_before, axis=1)
    slot_of = target_tile * capacity + earlier
    placing = jnp.arange(slot_count)[:, None] == slot_of[None, :]
    carried = {}

    def send_heat(halos):
        outgoing = jnp.dot(placing.astype(jnp.float32), heat, precision=HIGHEST_PRECISION)
        offsets = jnp.sum(jnp.where(placing, targets[None, :] + 1, 0), axis=1) - 1
        offset_row = jnp.zeros((tile_count, 1, out_width), jnp.float32).at[:, 0, :capacity].set(
            offsets.reshape(tile_count, capacity).astype(jnp.float32)
        )
        packet = jnp.concatenate([outgoing.reshape(tile_count, capacity, out_width), offset_row], axis=1)
        carried["packet"], halos = lax.optimization_barrier((packet, halos))
        return halos

    def warm_ocean(halos):
        arrived = lax.all_to_all(carried["packet"], "gx", split_axis=0, concat_axis=0, tiled=True)
        arrived_at = arrived[:, capacity, :capacity].reshape(slot_count).astype(jnp.int32)
        landing = jnp.arange(out_blocks)[:, None] == arrived_at[None, :]
        heating = jnp.dot(
            landing.astype(jnp.float32),
            arrived[:, :capacity].reshape(slot_count, out_width),
            precision=HIGHEST_PRECISION,
        )
        ocean_temp = ocean_st + ocean_wet * heating.reshape(cell_count)
        returning = jnp.dot(
            landing.T.astype(jnp.bfloat16),
            ocean_temp.astype(jnp.bfloat16).reshape(out_blocks, out_width),
            preferred_element_type=jnp.float32,
        ).astype(jnp.bfloat16)
        (carried["ocean"], carried["returning"]), halos = lax.optimization_barrier(
            ((ocean_temp, returning), halos)
        )
        return halos

    def return_temps(halos):
        delivered = lax.all_to_all(
            carried["returning"].reshape(tile_count, capacity, out_width), "gx", split_axis=0, concat_axis=0,
            tiled=True,
        )
        carried["delivered"], halos = lax.optimization_barrier((delivered, halos))
        return halos

    assert SUBSTEPS == 2
    p2, u2, v2 = stencil(
        pressure, eastward, northward, sound_speed, wetness, matrix, (send_heat, warm_ocean, return_temps)
    )
    final_state = jnp.stack([p2, u2, v2])[None]

    ocean_temp = carried["ocean"]
    per_pair = jnp.dot(
        placing.T.astype(jnp.bfloat16),
        carried["delivered"].reshape(slot_count, out_width),
        preferred_element_type=jnp.float32,
    ).astype(jnp.bfloat16)
    pieces = jnp.einsum("pio,po->pi", weights, per_pair, preferred_element_type=jnp.float32)
    owning = (jnp.arange(in_blocks)[:, None] == sources[None, :]).astype(jnp.float32)
    atmos_temp = jnp.dot(owning, pieces, precision=HIGHEST_PRECISION)

    surface_temps = jnp.where(is_atmos, atmos_temp.reshape(grid_shape), ocean_temp.reshape(grid_shape))[None]
    return (final_state, surface_temps)


def solution(mesh):
    return jax.shard_map(
        local,
        mesh=mesh,
        in_specs=(
            P("sec", None, None, "gx", "gy"),
            P("sec", "gx", "gy"),
            P("sec", "gx", "gy"),
            P("sec", None, None),
            P("sec", "gx", "gy"),
            P(),
            P(),
            P("gx", "gy", None, None),
            P("gx", "gy", None),
            P("gx", "gy", None),
            P("gx", "gy", None, None, None),
        ),
        out_specs=(P("sec", None, None, "gx", "gy"), P("sec", "gx", "gy")),
        check_vma=False,
    )
```

```python
import jax
import jax.numpy as jnp
from jax import lax
from jax.sharding import PartitionSpec as P

SUBSTEPS = 2


HIGHEST_PRECISION = lax.Precision.HIGHEST


def neighbours(head, tail, axis):
    count = lax.axis_size(axis)
    lo = lax.ppermute(tail, axis, [(i, i + 1) for i in range(count - 1)])
    hi = lax.ppermute(head, axis, [(i + 1, i) for i in range(count - 1)])
    return lo, hi


def neighbours_exchanged(head, tail, axis):
    count = lax.axis_size(axis)
    me = lax.axis_index(axis)
    ranks = jnp.arange(count).reshape((count,) + (1,) * head.ndim)
    sent = jnp.where(ranks == me - 1, head[None], jnp.where(ranks == me + 1, tail[None], 0.0))
    got = lax.all_to_all(sent, axis, 0, 0, tiled=True)
    lo = jnp.sum(jnp.where(ranks == me - 1, got, 0.0), axis=0)
    hi = jnp.sum(jnp.where(ranks == me + 1, got, 0.0), axis=0)
    return lo, hi


def vertical_mix(matrix, right_side):
    return right_side + jnp.einsum("lm,mxy->lxy", matrix, right_side, precision=HIGHEST_PRECISION)


def stencil(pressure, eastward, northward, sound_speed, wetness, matrix):
    wet3 = wetness[None]
    lo_x, hi_x = neighbours(
        jnp.concatenate([eastward[:, :1], wet3[:, :1]], axis=0),
        jnp.concatenate([eastward[:, -1:], wet3[:, -1:]], axis=0),
        "gx",
    )
    lo_y, hi_y = neighbours_exchanged(
        jnp.concatenate([northward[:, :, :1], wet3[:, :, :1]], axis=0),
        jnp.concatenate([northward[:, :, -1:], wet3[:, :, -1:]], axis=0),
        "gy",
    )
    levels = eastward.shape[0]
    u_ext = jnp.concatenate([lo_x[:levels], eastward, hi_x[:levels]], axis=1)
    wet_x = jnp.concatenate([lo_x[levels:], wet3, hi_x[levels:]], axis=1)
    v_ext = jnp.concatenate([lo_y[:levels], northward, hi_y[:levels]], axis=2)
    wet_y = jnp.concatenate([lo_y[levels:], wet3, hi_y[levels:]], axis=2)

    divergence = (u_ext[:, 2:] - u_ext[:, :-2]) + (v_ext[:, :, 2:] - v_ext[:, :, :-2])
    p1 = vertical_mix(matrix, pressure - sound_speed * divergence)

    lo2x, hi2x = neighbours(p1[:, :2], p1[:, -2:], "gx")
    lo2y, hi2y = neighbours_exchanged(p1[:, :, :2], p1[:, :, -2:], "gy")
    p1_x = jnp.concatenate([lo2x, p1, hi2x], axis=1)
    p1_y = jnp.concatenate([lo2y, p1, hi2y], axis=2)
    u1_ext = wet_x * (u_ext - 0.5 * (p1_x[:, 2:] - p1_x[:, :-2]))
    v1_ext = wet_y * (v_ext - 0.5 * (p1_y[:, :, 2:] - p1_y[:, :, :-2]))

    divergence = (u1_ext[:, 2:] - u1_ext[:, :-2]) + (v1_ext[:, :, 2:] - v1_ext[:, :, :-2])
    p2 = vertical_mix(matrix, p1 - sound_speed * divergence)

    lo3x, hi3x = neighbours(p2[:, :1], p2[:, -1:], "gx")
    lo3y, hi3y = neighbours_exchanged(p2[:, :, :1], p2[:, :, -1:], "gy")
    p2_x = jnp.concatenate([lo3x, p2, hi3x], axis=1)
    p2_y = jnp.concatenate([lo3y, p2, hi3y], axis=2)
    u1 = u1_ext[:, 1:-1]
    v1 = v1_ext[:, :, 1:-1]
    u2 = wetness * (u1 - 0.5 * (p2_x[:, 2:] - p2_x[:, :-2]))
    v2 = wetness * (v1 - 0.5 * (p2_y[:, :, 2:] - p2_y[:, :, :-2]))
    return p2, u2, v2


def local(
    model_state,
    wave_speed,
    wet_mask,
    vertical,
    surface_temp,
    flux_coef,
    heat_gain,
    pair_tile,
    pair_source,
    pair_target,
    intersection_weights,
):
    pressure = model_state[0, 0]
    eastward = model_state[0, 1]
    northward = model_state[0, 2]
    sound_speed = wave_speed[0]
    wetness = wet_mask[0].astype(jnp.float32)
    matrix = vertical[0]
    assert SUBSTEPS == 2
    p2, u2, v2 = stencil(pressure, eastward, northward, sound_speed, wetness, matrix)
    final_state = jnp.stack([p2, u2, v2])[None]

    weights = intersection_weights[0, 0]
    pair_count, in_width, out_width = weights.shape
    tile_count = lax.axis_size("gx")
    grid_shape = surface_temp.shape[1:]
    cell_count = grid_shape[0] * grid_shape[1]
    in_blocks = cell_count // in_width
    out_blocks = cell_count // out_width
    sources = pair_source[0, 0]
    targets = pair_target[0, 0]
    target_tile = pair_tile[0, 0, :, 0]
    is_atmos = lax.axis_index("sec") == 0

    own_st = surface_temp[0].reshape(cell_count)
    own_wet = wetness.reshape(cell_count)
    drivers = jnp.stack(
        [model_state[0, 0, 0].reshape(cell_count), model_state[0, 1, 0].reshape(cell_count),
         model_state[0, 2, 0].reshape(cell_count), own_st]
    )
    zeros = jnp.zeros_like(own_st)
    sent = jnp.where(is_atmos, drivers, jnp.stack([own_st, own_wet, zeros, zeros]))
    got = lax.ppermute(sent, "sec", [(0, 1), (1, 0)])
    atmos_drivers = jnp.where(is_atmos, drivers, got)
    ocean_st = jnp.where(is_atmos, got[0], own_st)
    ocean_wet = jnp.where(is_atmos, got[1], own_wet)

    fluxes = jnp.tanh(jnp.dot(flux_coef, atmos_drivers, precision=HIGHEST_PRECISION)).astype(jnp.bfloat16)
    flux_count = fluxes.shape[0]
    blocks = fluxes.reshape(flux_count, in_blocks, in_width)
    picked = jnp.take(blocks, sources, axis=1)
    regridded = jnp.einsum(
        "fpi,pio->pfo", picked, weights, preferred_element_type=jnp.float32
    ).astype(jnp.bfloat16)
    heat = jnp.einsum(
        "f,pfo->po", heat_gain, regridded.astype(jnp.float32), precision=HIGHEST_PRECISION
    )

    capacity = max(2, 2 * pair_count // tile_count)
    slot_count = tile_count * capacity
    positions = jnp.arange(pair_count)
    same_tile = target_tile[None, :] == target_tile[:, None]
    is_before = positions[None, :] < positions[:, None]
    earlier = jnp.sum(same_tile & is_before, axis=1)
    slot_of = target_tile * capacity + earlier
    placing = jnp.arange(slot_count)[:, None] == slot_of[None, :]
    outgoing = jnp.dot(placing.astype(jnp.float32), heat, precision=HIGHEST_PRECISION)
    offsets = jnp.sum(jnp.where(placing, targets[None, :] + 1, 0), axis=1) - 1
    offset_row = jnp.zeros((tile_count, 1, out_width), jnp.float32).at[:, 0, :capacity].set(
        offsets.reshape(tile_count, capacity).astype(jnp.float32)
    )
    packet = jnp.concatenate([outgoing.reshape(tile_count, capacity, out_width), offset_row], axis=1)
    arrived = lax.all_to_all(packet, "gx", split_axis=0, concat_axis=0, tiled=True)
    arrived_at = arrived[:, capacity, :capacity].reshape(slot_count).astype(jnp.int32)
    landing = jnp.arange(out_blocks)[:, None] == arrived_at[None, :]
    heating = jnp.dot(
        landing.astype(jnp.float32),
        arrived[:, :capacity].reshape(slot_count, out_width),
        precision=HIGHEST_PRECISION,
    )
    ocean_temp = ocean_st + ocean_wet * heating.reshape(cell_count)

    returning = jnp.dot(
        landing.T.astype(jnp.bfloat16),
        ocean_temp.astype(jnp.bfloat16).reshape(out_blocks, out_width),
        preferred_element_type=jnp.float32,
    ).astype(jnp.bfloat16)
    delivered = lax.all_to_all(
        returning.reshape(tile_count, capacity, out_width), "gx", split_axis=0, concat_axis=0, tiled=True
    )
    per_pair = jnp.dot(
        placing.T.astype(jnp.bfloat16),
        delivered.reshape(slot_count, out_width),
        preferred_element_type=jnp.float32,
    ).astype(jnp.bfloat16)
    pieces = jnp.einsum("pio,po->pi", weights, per_pair, preferred_element_type=jnp.float32)
    owning = (jnp.arange(in_blocks)[:, None] == sources[None, :]).astype(jnp.float32)
    atmos_temp = jnp.dot(owning, pieces, precision=HIGHEST_PRECISION)

    surface_temps = jnp.where(is_atmos, atmos_temp.reshape(grid_shape), ocean_temp.reshape(grid_shape))[None]
    return (final_state, surface_temps)


def solution(mesh):
    return jax.shard_map(
        local,
        mesh=mesh,
        in_specs=(
            P("sec", None, None, "gx", "gy"),
            P("sec", "gx", "gy"),
            P("sec", "gx", "gy"),
            P("sec", None, None),
            P("sec", "gx", "gy"),
            P(),
            P(),
            P("gx", "gy", None, None),
            P("gx", "gy", None),
            P("gx", "gy", None),
            P("gx", "gy", None, None, None),
        ),
        out_specs=(P("sec", None, None, "gx", "gy"), P("sec", "gx", "gy")),
        check_vma=False,
    )
```

```python
import jax
import jax.numpy as jnp
from jax import lax
from jax.sharding import PartitionSpec as P

SUBSTEPS = 2


HIGHEST_PRECISION = lax.Precision.HIGHEST


def neighbours(head, tail, axis):
    count = lax.axis_size(axis)
    lo = lax.ppermute(tail, axis, [(i, i + 1) for i in range(count - 1)])
    hi = lax.ppermute(head, axis, [(i + 1, i) for i in range(count - 1)])
    return lo, hi


def vertical_mix(matrix, right_side):
    return right_side + jnp.einsum("lm,mxy->lxy", matrix, right_side, precision=HIGHEST_PRECISION)


def stencil(pressure, eastward, northward, sound_speed, wetness, matrix):
    wet3 = wetness[None]
    lo_x, hi_x = neighbours(
        jnp.concatenate([eastward[:, :1], wet3[:, :1]], axis=0),
        jnp.concatenate([eastward[:, -1:], wet3[:, -1:]], axis=0),
        "gx",
    )
    lo_y, hi_y = neighbours(
        jnp.concatenate([northward[:, :, :1], wet3[:, :, :1]], axis=0),
        jnp.concatenate([northward[:, :, -1:], wet3[:, :, -1:]], axis=0),
        "gy",
    )
    levels = eastward.shape[0]
    u_ext = jnp.concatenate([lo_x[:levels], eastward, hi_x[:levels]], axis=1)
    wet_x = jnp.concatenate([lo_x[levels:], wet3, hi_x[levels:]], axis=1)
    v_ext = jnp.concatenate([lo_y[:levels], northward, hi_y[:levels]], axis=2)
    wet_y = jnp.concatenate([lo_y[levels:], wet3, hi_y[levels:]], axis=2)

    divergence = (u_ext[:, 2:] - u_ext[:, :-2]) + (v_ext[:, :, 2:] - v_ext[:, :, :-2])
    p1 = vertical_mix(matrix, pressure - sound_speed * divergence)

    lo2x, hi2x = neighbours(p1[:, :2], p1[:, -2:], "gx")
    lo2y, hi2y = neighbours(p1[:, :, :2], p1[:, :, -2:], "gy")
    p1_x = jnp.concatenate([lo2x, p1, hi2x], axis=1)
    p1_y = jnp.concatenate([lo2y, p1, hi2y], axis=2)
    u1_ext = wet_x * (u_ext - 0.5 * (p1_x[:, 2:] - p1_x[:, :-2]))
    v1_ext = wet_y * (v_ext - 0.5 * (p1_y[:, :, 2:] - p1_y[:, :, :-2]))

    divergence = (u1_ext[:, 2:] - u1_ext[:, :-2]) + (v1_ext[:, :, 2:] - v1_ext[:, :, :-2])
    p2 = vertical_mix(matrix, p1 - sound_speed * divergence)

    lo3x, hi3x = neighbours(p2[:, :1], p2[:, -1:], "gx")
    lo3y, hi3y = neighbours(p2[:, :, :1], p2[:, :, -1:], "gy")
    p2_x = jnp.concatenate([lo3x, p2, hi3x], axis=1)
    p2_y = jnp.concatenate([lo3y, p2, hi3y], axis=2)
    u1 = u1_ext[:, 1:-1]
    v1 = v1_ext[:, :, 1:-1]
    u2 = wetness * (u1 - 0.5 * (p2_x[:, 2:] - p2_x[:, :-2]))
    v2 = wetness * (v1 - 0.5 * (p2_y[:, :, 2:] - p2_y[:, :, :-2]))
    return p2, u2, v2


def local(
    model_state,
    wave_speed,
    wet_mask,
    vertical,
    surface_temp,
    flux_coef,
    heat_gain,
    pair_tile,
    pair_source,
    pair_target,
    intersection_weights,
):
    pressure = model_state[0, 0]
    eastward = model_state[0, 1]
    northward = model_state[0, 2]
    sound_speed = wave_speed[0]
    wetness = wet_mask[0].astype(jnp.float32)
    matrix = vertical[0]

    weights = intersection_weights[0, 0]
    pair_count, in_width, out_width = weights.shape
    tile_count = lax.axis_size("gx")
    grid_shape = surface_temp.shape[1:]
    cell_count = grid_shape[0] * grid_shape[1]
    in_blocks = cell_count // in_width
    out_blocks = cell_count // out_width
    sources = pair_source[0, 0]
    targets = pair_target[0, 0]
    target_tile = pair_tile[0, 0, :, 0]
    is_atmos = lax.axis_index("sec") == 0

    own_st = surface_temp[0].reshape(cell_count)
    own_wet = wetness.reshape(cell_count)
    got = lax.ppermute(jnp.stack([own_st, own_wet]), "sec", [(1, 0)])
    ocean_st = got[0]
    ocean_wet = got[1]
    atmos_drivers = jnp.stack(
        [model_state[0, 0, 0].reshape(cell_count), model_state[0, 1, 0].reshape(cell_count),
         model_state[0, 2, 0].reshape(cell_count), own_st]
    )

    fluxes = jnp.tanh(jnp.dot(flux_coef, atmos_drivers, precision=HIGHEST_PRECISION)).astype(jnp.bfloat16)
    flux_count = fluxes.shape[0]
    blocks = fluxes.reshape(flux_count, in_blocks, in_width)
    picked = jnp.take(blocks, sources, axis=1)
    regridded = jnp.einsum(
        "fpi,pio->pfo", picked, weights, preferred_element_type=jnp.float32
    ).astype(jnp.bfloat16)
    heat = jnp.einsum(
        "f,pfo->po", heat_gain, regridded.astype(jnp.float32), precision=HIGHEST_PRECISION
    )

    capacity = max(2, 2 * pair_count // tile_count)
    slot_count = tile_count * capacity
    positions = jnp.arange(pair_count)
    same_tile = target_tile[None, :] == target_tile[:, None]
    is_before = positions[None, :] < positions[:, None]
    earlier = jnp.sum(same_tile & is_before, axis=1)
    slot_of = target_tile * capacity + earlier
    placing = jnp.arange(slot_count)[:, None] == slot_of[None, :]
    outgoing = jnp.dot(placing.astype(jnp.float32), heat, precision=HIGHEST_PRECISION)
    offsets = jnp.sum(jnp.where(placing, targets[None, :] + 1, 0), axis=1) - 1
    offset_row = jnp.zeros((tile_count, 1, out_width), jnp.float32).at[:, 0, :capacity].set(
        offsets.reshape(tile_count, capacity).astype(jnp.float32)
    )
    packet = jnp.concatenate([outgoing.reshape(tile_count, capacity, out_width), offset_row], axis=1)
    arrived = lax.all_to_all(packet, "gx", split_axis=0, concat_axis=0, tiled=True)
    arrived, pressure, eastward, northward = lax.optimization_barrier((arrived, pressure, eastward, northward))
    assert SUBSTEPS == 2
    p2, u2, v2 = stencil(pressure, eastward, northward, sound_speed, wetness, matrix)
    final_state = jnp.stack([p2, u2, v2])[None]
    arrived_at = arrived[:, capacity, :capacity].reshape(slot_count).astype(jnp.int32)
    landing = jnp.arange(out_blocks)[:, None] == arrived_at[None, :]
    heating = jnp.dot(
        landing.astype(jnp.float32),
        arrived[:, :capacity].reshape(slot_count, out_width),
        precision=HIGHEST_PRECISION,
    )
    ocean_temp = ocean_st + ocean_wet * heating.reshape(cell_count)

    returning = jnp.dot(
        landing.T.astype(jnp.bfloat16),
        ocean_temp.astype(jnp.bfloat16).reshape(out_blocks, out_width),
        preferred_element_type=jnp.float32,
    ).astype(jnp.bfloat16)
    delivered = lax.all_to_all(
        returning.reshape(tile_count, capacity, out_width), "gx", split_axis=0, concat_axis=0, tiled=True
    )
    per_pair = jnp.dot(
        placing.T.astype(jnp.bfloat16),
        delivered.reshape(slot_count, out_width),
        preferred_element_type=jnp.float32,
    ).astype(jnp.bfloat16)
    pieces = jnp.einsum("pio,po->pi", weights, per_pair, preferred_element_type=jnp.float32)
    owning = (jnp.arange(in_blocks)[:, None] == sources[None, :]).astype(jnp.float32)
    atmos_temp = jnp.dot(owning, pieces, precision=HIGHEST_PRECISION)

    ocean_back = lax.ppermute(ocean_temp, "sec", [(0, 1)])
    surface_temps = jnp.where(is_atmos, atmos_temp.reshape(grid_shape), ocean_back.reshape(grid_shape))[None]
    return (final_state, surface_temps)


def solution(mesh):
    return jax.shard_map(
        local,
        mesh=mesh,
        in_specs=(
            P("sec", None, None, "gx", "gy"),
            P("sec", "gx", "gy"),
            P("sec", "gx", "gy"),
            P("sec", None, None),
            P("sec", "gx", "gy"),
            P(),
            P(),
            P("gx", "gy", None, None),
            P("gx", "gy", None),
            P("gx", "gy", None),
            P("gx", "gy", None, None, None),
        ),
        out_specs=(P("sec", None, None, "gx", "gy"), P("sec", "gx", "gy")),
        check_vma=False,
    )
```

```python
import jax
import jax.numpy as jnp
from jax import lax
from jax.sharding import PartitionSpec as P

SUBSTEPS = 2


HIGHEST_PRECISION = lax.Precision.HIGHEST


def neighbours(head, tail, axis):
    count = lax.axis_size(axis)
    lo = lax.ppermute(tail, axis, [(i, i + 1) for i in range(count - 1)])
    hi = lax.ppermute(head, axis, [(i + 1, i) for i in range(count - 1)])
    return lo, hi


def vertical_mix(matrix, right_side):
    return right_side + jnp.einsum("lm,mxy->lxy", matrix, right_side, precision=HIGHEST_PRECISION)


def stencil(pressure, eastward, northward, sound_speed, wetness, matrix):
    wet3 = wetness[None]
    lo_x, hi_x = neighbours(
        jnp.concatenate([eastward[:, :1], wet3[:, :1]], axis=0),
        jnp.concatenate([eastward[:, -1:], wet3[:, -1:]], axis=0),
        "gx",
    )
    lo_y, hi_y = neighbours(
        jnp.concatenate([northward[:, :, :1], wet3[:, :, :1]], axis=0),
        jnp.concatenate([northward[:, :, -1:], wet3[:, :, -1:]], axis=0),
        "gy",
    )
    levels = eastward.shape[0]
    u_ext = jnp.concatenate([lo_x[:levels], eastward, hi_x[:levels]], axis=1)
    wet_x = jnp.concatenate([lo_x[levels:], wet3, hi_x[levels:]], axis=1)
    v_ext = jnp.concatenate([lo_y[:levels], northward, hi_y[:levels]], axis=2)
    wet_y = jnp.concatenate([lo_y[levels:], wet3, hi_y[levels:]], axis=2)

    divergence = (u_ext[:, 2:] - u_ext[:, :-2]) + (v_ext[:, :, 2:] - v_ext[:, :, :-2])
    p1 = vertical_mix(matrix, pressure - sound_speed * divergence)

    lo2x, hi2x = neighbours(p1[:, :2], p1[:, -2:], "gx")
    lo2y, hi2y = neighbours(p1[:, :, :2], p1[:, :, -2:], "gy")
    p1_x = jnp.concatenate([lo2x, p1, hi2x], axis=1)
    p1_y = jnp.concatenate([lo2y, p1, hi2y], axis=2)
    u1_ext = wet_x * (u_ext - 0.5 * (p1_x[:, 2:] - p1_x[:, :-2]))
    v1_ext = wet_y * (v_ext - 0.5 * (p1_y[:, :, 2:] - p1_y[:, :, :-2]))

    divergence = (u1_ext[:, 2:] - u1_ext[:, :-2]) + (v1_ext[:, :, 2:] - v1_ext[:, :, :-2])
    p2 = vertical_mix(matrix, p1 - sound_speed * divergence)

    lo3x, hi3x = neighbours(p2[:, :1], p2[:, -1:], "gx")
    lo3y, hi3y = neighbours(p2[:, :, :1], p2[:, :, -1:], "gy")
    p2_x = jnp.concatenate([lo3x, p2, hi3x], axis=1)
    p2_y = jnp.concatenate([lo3y, p2, hi3y], axis=2)
    u1 = u1_ext[:, 1:-1]
    v1 = v1_ext[:, :, 1:-1]
    u2 = wetness * (u1 - 0.5 * (p2_x[:, 2:] - p2_x[:, :-2]))
    v2 = wetness * (v1 - 0.5 * (p2_y[:, :, 2:] - p2_y[:, :, :-2]))
    return p2, u2, v2


def local(
    model_state,
    wave_speed,
    wet_mask,
    vertical,
    surface_temp,
    flux_coef,
    heat_gain,
    pair_tile,
    pair_source,
    pair_target,
    intersection_weights,
):
    pressure = model_state[0, 0]
    eastward = model_state[0, 1]
    northward = model_state[0, 2]
    sound_speed = wave_speed[0]
    wetness = wet_mask[0].astype(jnp.float32)
    matrix = vertical[0]

    weights = intersection_weights[0, 0]
    pair_count, in_width, out_width = weights.shape
    tile_count = lax.axis_size("gx")
    grid_shape = surface_temp.shape[1:]
    cell_count = grid_shape[0] * grid_shape[1]
    in_blocks = cell_count // in_width
    out_blocks = cell_count // out_width
    sources = pair_source[0, 0]
    targets = pair_target[0, 0]
    target_tile = pair_tile[0, 0, :, 0]
    is_atmos = lax.axis_index("sec") == 0

    own_st = surface_temp[0].reshape(cell_count)
    own_wet = wetness.reshape(cell_count)
    got = lax.ppermute(jnp.stack([own_st, own_wet]), "sec", [(1, 0)])
    ocean_st = got[0]
    ocean_wet = got[1]
    atmos_drivers = jnp.stack(
        [model_state[0, 0, 0].reshape(cell_count), model_state[0, 1, 0].reshape(cell_count),
         model_state[0, 2, 0].reshape(cell_count), own_st]
    )

    fluxes = jnp.tanh(jnp.dot(flux_coef, atmos_drivers, precision=HIGHEST_PRECISION)).astype(jnp.bfloat16)
    flux_count = fluxes.shape[0]
    blocks = fluxes.reshape(flux_count, in_blocks, in_width)
    picked = jnp.take(blocks, sources, axis=1)
    regridded = jnp.einsum(
        "fpi,pio->pfo", picked, weights, preferred_element_type=jnp.float32
    ).astype(jnp.bfloat16)
    heat = jnp.einsum(
        "f,pfo->po", heat_gain, regridded.astype(jnp.float32), precision=HIGHEST_PRECISION
    )

    capacity = max(2, 2 * pair_count // tile_count)
    slot_count = tile_count * capacity
    positions = jnp.arange(pair_count)
    same_tile = target_tile[None, :] == target_tile[:, None]
    is_before = positions[None, :] < positions[:, None]
    earlier = jnp.sum(same_tile & is_before, axis=1)
    slot_of = target_tile * capacity + earlier
    placing = jnp.arange(slot_count)[:, None] == slot_of[None, :]
    outgoing = jnp.dot(placing.astype(jnp.float32), heat, precision=HIGHEST_PRECISION)
    offsets = jnp.sum(jnp.where(placing, targets[None, :] + 1, 0), axis=1) - 1
    offset_row = jnp.zeros((tile_count, 1, out_width), jnp.float32).at[:, 0, :capacity].set(
        offsets.reshape(tile_count, capacity).astype(jnp.float32)
    )
    packet = jnp.concatenate([outgoing.reshape(tile_count, capacity, out_width), offset_row], axis=1)
    arrived = lax.all_to_all(packet, "gx", split_axis=0, concat_axis=0, tiled=True)
    arrived, pressure = lax.optimization_barrier((arrived, pressure))
    assert SUBSTEPS == 2
    p2, u2, v2 = stencil(pressure, eastward, northward, sound_speed, wetness, matrix)
    final_state = jnp.stack([p2, u2, v2])[None]
    arrived_at = arrived[:, capacity, :capacity].reshape(slot_count).astype(jnp.int32)
    landing = jnp.arange(out_blocks)[:, None] == arrived_at[None, :]
    heating = jnp.dot(
        landing.astype(jnp.float32),
        arrived[:, :capacity].reshape(slot_count, out_width),
        precision=HIGHEST_PRECISION,
    )
    ocean_temp = ocean_st + ocean_wet * heating.reshape(cell_count)

    returning = jnp.dot(
        landing.T.astype(jnp.bfloat16),
        ocean_temp.astype(jnp.bfloat16).reshape(out_blocks, out_width),
        preferred_element_type=jnp.float32,
    ).astype(jnp.bfloat16)
    delivered = lax.all_to_all(
        returning.reshape(tile_count, capacity, out_width), "gx", split_axis=0, concat_axis=0, tiled=True
    )
    per_pair = jnp.dot(
        placing.T.astype(jnp.bfloat16),
        delivered.reshape(slot_count, out_width),
        preferred_element_type=jnp.float32,
    ).astype(jnp.bfloat16)
    pieces = jnp.einsum("pio,po->pi", weights, per_pair, preferred_element_type=jnp.float32)
    owning = (jnp.arange(in_blocks)[:, None] == sources[None, :]).astype(jnp.float32)
    atmos_temp = jnp.dot(owning, pieces, precision=HIGHEST_PRECISION)

    ocean_back = lax.ppermute(ocean_temp, "sec", [(0, 1)])
    surface_temps = jnp.where(is_atmos, atmos_temp.reshape(grid_shape), ocean_back.reshape(grid_shape))[None]
    return (final_state, surface_temps)


def solution(mesh):
    return jax.shard_map(
        local,
        mesh=mesh,
        in_specs=(
            P("sec", None, None, "gx", "gy"),
            P("sec", "gx", "gy"),
            P("sec", "gx", "gy"),
            P("sec", None, None),
            P("sec", "gx", "gy"),
            P(),
            P(),
            P("gx", "gy", None, None),
            P("gx", "gy", None),
            P("gx", "gy", None),
            P("gx", "gy", None, None, None),
        ),
        out_specs=(P("sec", None, None, "gx", "gy"), P("sec", "gx", "gy")),
        check_vma=False,
    )
```

```python
import jax
import jax.numpy as jnp
from jax import lax
from jax.sharding import PartitionSpec as P

SUBSTEPS = 2


HIGHEST_PRECISION = lax.Precision.HIGHEST


def neighbours(head, tail, axis):
    count = lax.axis_size(axis)
    lo = lax.ppermute(tail, axis, [(i, i + 1) for i in range(count - 1)])
    hi = lax.ppermute(head, axis, [(i + 1, i) for i in range(count - 1)])
    return lo, hi


def vertical_mix(matrix, right_side):
    return right_side + jnp.einsum("lm,mxy->lxy", matrix, right_side, precision=HIGHEST_PRECISION)


def stencil(pressure, eastward, northward, sound_speed, wetness, matrix):
    wet3 = wetness[None]
    lo_x, hi_x = neighbours(
        jnp.concatenate([eastward[:, :1], wet3[:, :1]], axis=0),
        jnp.concatenate([eastward[:, -1:], wet3[:, -1:]], axis=0),
        "gx",
    )
    lo_y, hi_y = neighbours(
        jnp.concatenate([northward[:, :, :1], wet3[:, :, :1]], axis=0),
        jnp.concatenate([northward[:, :, -1:], wet3[:, :, -1:]], axis=0),
        "gy",
    )
    levels = eastward.shape[0]
    u_ext = jnp.concatenate([lo_x[:levels], eastward, hi_x[:levels]], axis=1)
    wet_x = jnp.concatenate([lo_x[levels:], wet3, hi_x[levels:]], axis=1)
    v_ext = jnp.concatenate([lo_y[:levels], northward, hi_y[:levels]], axis=2)
    wet_y = jnp.concatenate([lo_y[levels:], wet3, hi_y[levels:]], axis=2)

    divergence = (u_ext[:, 2:] - u_ext[:, :-2]) + (v_ext[:, :, 2:] - v_ext[:, :, :-2])
    p1 = vertical_mix(matrix, pressure - sound_speed * divergence)

    lo2x, hi2x = neighbours(p1[:, :2], p1[:, -2:], "gx")
    lo2y, hi2y = neighbours(p1[:, :, :2], p1[:, :, -2:], "gy")
    p1_x = jnp.concatenate([lo2x, p1, hi2x], axis=1)
    p1_y = jnp.concatenate([lo2y, p1, hi2y], axis=2)
    u1_ext = wet_x * (u_ext - 0.5 * (p1_x[:, 2:] - p1_x[:, :-2]))
    v1_ext = wet_y * (v_ext - 0.5 * (p1_y[:, :, 2:] - p1_y[:, :, :-2]))

    divergence = (u1_ext[:, 2:] - u1_ext[:, :-2]) + (v1_ext[:, :, 2:] - v1_ext[:, :, :-2])
    p2 = vertical_mix(matrix, p1 - sound_speed * divergence)

    lo3x, hi3x = neighbours(p2[:, :1], p2[:, -1:], "gx")
    lo3y, hi3y = neighbours(p2[:, :, :1], p2[:, :, -1:], "gy")
    p2_x = jnp.concatenate([lo3x, p2, hi3x], axis=1)
    p2_y = jnp.concatenate([lo3y, p2, hi3y], axis=2)
    u1 = u1_ext[:, 1:-1]
    v1 = v1_ext[:, :, 1:-1]
    u2 = wetness * (u1 - 0.5 * (p2_x[:, 2:] - p2_x[:, :-2]))
    v2 = wetness * (v1 - 0.5 * (p2_y[:, :, 2:] - p2_y[:, :, :-2]))
    return p2, u2, v2


def local(
    model_state,
    wave_speed,
    wet_mask,
    vertical,
    surface_temp,
    flux_coef,
    heat_gain,
    pair_tile,
    pair_source,
    pair_target,
    intersection_weights,
):
    pressure = model_state[0, 0]
    eastward = model_state[0, 1]
    northward = model_state[0, 2]
    sound_speed = wave_speed[0]
    wetness = wet_mask[0].astype(jnp.float32)
    matrix = vertical[0]

    weights = intersection_weights[0, 0]
    pair_count, in_width, out_width = weights.shape
    tile_count = lax.axis_size("gx")
    grid_shape = surface_temp.shape[1:]
    cell_count = grid_shape[0] * grid_shape[1]
    in_blocks = cell_count // in_width
    out_blocks = cell_count // out_width
    sources = pair_source[0, 0]
    targets = pair_target[0, 0]
    target_tile = pair_tile[0, 0, :, 0]
    is_atmos = lax.axis_index("sec") == 0

    own_st = surface_temp[0].reshape(cell_count)
    own_wet = wetness.reshape(cell_count)
    drivers = jnp.stack(
        [model_state[0, 0, 0].reshape(cell_count), model_state[0, 1, 0].reshape(cell_count),
         model_state[0, 2, 0].reshape(cell_count), own_st]
    )
    zeros = jnp.zeros_like(own_st)
    sent = jnp.where(is_atmos, drivers, jnp.stack([own_st, own_wet, zeros, zeros]))
    got = lax.ppermute(sent, "sec", [(0, 1), (1, 0)])
    atmos_drivers = jnp.where(is_atmos, drivers, got)
    ocean_st = jnp.where(is_atmos, got[0], own_st)
    ocean_wet = jnp.where(is_atmos, got[1], own_wet)

    fluxes = jnp.tanh(jnp.dot(flux_coef, atmos_drivers, precision=HIGHEST_PRECISION)).astype(jnp.bfloat16)
    flux_count = fluxes.shape[0]
    blocks = fluxes.reshape(flux_count, in_blocks, in_width)
    picked = jnp.take(blocks, sources, axis=1)
    regridded = jnp.einsum(
        "fpi,pio->pfo", picked, weights, preferred_element_type=jnp.float32
    ).astype(jnp.bfloat16)
    heat = jnp.einsum(
        "f,pfo->po", heat_gain, regridded.astype(jnp.float32), precision=HIGHEST_PRECISION
    )

    capacity = max(2, 2 * pair_count // tile_count)
    slot_count = tile_count * capacity
    positions = jnp.arange(pair_count)
    same_tile = target_tile[None, :] == target_tile[:, None]
    is_before = positions[None, :] < positions[:, None]
    earlier = jnp.sum(same_tile & is_before, axis=1)
    slot_of = target_tile * capacity + earlier
    placing = jnp.arange(slot_count)[:, None] == slot_of[None, :]
    outgoing = jnp.dot(placing.astype(jnp.float32), heat, precision=HIGHEST_PRECISION)
    offsets = jnp.sum(jnp.where(placing, targets[None, :] + 1, 0), axis=1) - 1
    offset_row = jnp.zeros((tile_count, 1, out_width), jnp.float32).at[:, 0, :capacity].set(
        offsets.reshape(tile_count, capacity).astype(jnp.float32)
    )
    packet = jnp.concatenate([outgoing.reshape(tile_count, capacity, out_width), offset_row], axis=1)
    arrived = lax.all_to_all(packet, "gx", split_axis=0, concat_axis=0, tiled=True)
    arrived, pressure, eastward, northward = lax.optimization_barrier((arrived, pressure, eastward, northward))
    assert SUBSTEPS == 2
    p2, u2, v2 = stencil(pressure, eastward, northward, sound_speed, wetness, matrix)
    final_state = jnp.stack([p2, u2, v2])[None]
    arrived_at = arrived[:, capacity, :capacity].reshape(slot_count).astype(jnp.int32)
    landing = jnp.arange(out_blocks)[:, None] == arrived_at[None, :]
    heating = jnp.dot(
        landing.astype(jnp.float32),
        arrived[:, :capacity].reshape(slot_count, out_width),
        precision=HIGHEST_PRECISION,
    )
    ocean_temp = ocean_st + ocean_wet * heating.reshape(cell_count)

    returning = jnp.dot(
        landing.T.astype(jnp.bfloat16),
        ocean_temp.astype(jnp.bfloat16).reshape(out_blocks, out_width),
        preferred_element_type=jnp.float32,
    ).astype(jnp.bfloat16)
    delivered = lax.all_to_all(
        returning.reshape(tile_count, capacity, out_width), "gx", split_axis=0, concat_axis=0, tiled=True
    )
    per_pair = jnp.dot(
        placing.T.astype(jnp.bfloat16),
        delivered.reshape(slot_count, out_width),
        preferred_element_type=jnp.float32,
    ).astype(jnp.bfloat16)
    pieces = jnp.einsum("pio,po->pi", weights, per_pair, preferred_element_type=jnp.float32)
    owning = (jnp.arange(in_blocks)[:, None] == sources[None, :]).astype(jnp.float32)
    atmos_temp = jnp.dot(owning, pieces, precision=HIGHEST_PRECISION)

    surface_temps = jnp.where(is_atmos, atmos_temp.reshape(grid_shape), ocean_temp.reshape(grid_shape))[None]
    return (final_state, surface_temps)


def solution(mesh):
    return jax.shard_map(
        local,
        mesh=mesh,
        in_specs=(
            P("sec", None, None, "gx", "gy"),
            P("sec", "gx", "gy"),
            P("sec", "gx", "gy"),
            P("sec", None, None),
            P("sec", "gx", "gy"),
            P(),
            P(),
            P("gx", "gy", None, None),
            P("gx", "gy", None),
            P("gx", "gy", None),
            P("gx", "gy", None, None, None),
        ),
        out_specs=(P("sec", None, None, "gx", "gy"), P("sec", "gx", "gy")),
        check_vma=False,
    )
```

```python
import jax
import jax.numpy as jnp
from jax import lax
from jax.sharding import PartitionSpec as P

SUBSTEPS = 2


HIGHEST_PRECISION = lax.Precision.HIGHEST


def neighbours(head, tail, axis):
    count = lax.axis_size(axis)
    lo = lax.ppermute(tail, axis, [(i, i + 1) for i in range(count - 1)])
    hi = lax.ppermute(head, axis, [(i + 1, i) for i in range(count - 1)])
    return lo, hi


def vertical_mix(matrix, right_side):
    return right_side + jnp.einsum("lm,mxy->lxy", matrix, right_side, precision=HIGHEST_PRECISION)


def stencil(pressure, eastward, northward, sound_speed, wetness, matrix, tie):
    wet3 = wetness[None]
    lo_x, hi_x = neighbours(
        jnp.concatenate([eastward[:, :1], wet3[:, :1]], axis=0),
        jnp.concatenate([eastward[:, -1:], wet3[:, -1:]], axis=0),
        "gx",
    )
    lo_y, hi_y = neighbours(
        jnp.concatenate([northward[:, :, :1], wet3[:, :, :1]], axis=0),
        jnp.concatenate([northward[:, :, -1:], wet3[:, :, -1:]], axis=0),
        "gy",
    )
    levels = eastward.shape[0]
    u_ext = jnp.concatenate([lo_x[:levels], eastward, hi_x[:levels]], axis=1)
    wet_x = jnp.concatenate([lo_x[levels:], wet3, hi_x[levels:]], axis=1)
    v_ext = jnp.concatenate([lo_y[:levels], northward, hi_y[:levels]], axis=2)
    wet_y = jnp.concatenate([lo_y[levels:], wet3, hi_y[levels:]], axis=2)

    divergence = (u_ext[:, 2:] - u_ext[:, :-2]) + (v_ext[:, :, 2:] - v_ext[:, :, :-2])
    p1 = vertical_mix(matrix, pressure - sound_speed * divergence)

    lo2x, hi2x = neighbours(p1[:, :2], p1[:, -2:], "gx")
    lo2y, hi2y = neighbours(p1[:, :, :2], p1[:, :, -2:], "gy")
    p1_x = jnp.concatenate([lo2x, p1, hi2x], axis=1)
    p1_y = jnp.concatenate([lo2y, p1, hi2y], axis=2)
    u1_ext = wet_x * (u_ext - 0.5 * (p1_x[:, 2:] - p1_x[:, :-2]))
    v1_ext = wet_y * (v_ext - 0.5 * (p1_y[:, :, 2:] - p1_y[:, :, :-2]))

    divergence = (u1_ext[:, 2:] - u1_ext[:, :-2]) + (v1_ext[:, :, 2:] - v1_ext[:, :, :-2])
    p2 = tie(vertical_mix(matrix, p1 - sound_speed * divergence))

    lo3x, hi3x = neighbours(p2[:, :1], p2[:, -1:], "gx")
    lo3y, hi3y = neighbours(p2[:, :, :1], p2[:, :, -1:], "gy")
    p2_x = jnp.concatenate([lo3x, p2, hi3x], axis=1)
    p2_y = jnp.concatenate([lo3y, p2, hi3y], axis=2)
    u1 = u1_ext[:, 1:-1]
    v1 = v1_ext[:, :, 1:-1]
    u2 = wetness * (u1 - 0.5 * (p2_x[:, 2:] - p2_x[:, :-2]))
    v2 = wetness * (v1 - 0.5 * (p2_y[:, :, 2:] - p2_y[:, :, :-2]))
    return p2, u2, v2


def local(
    model_state,
    wave_speed,
    wet_mask,
    vertical,
    surface_temp,
    flux_coef,
    heat_gain,
    pair_tile,
    pair_source,
    pair_target,
    intersection_weights,
):
    pressure = model_state[0, 0]
    eastward = model_state[0, 1]
    northward = model_state[0, 2]
    sound_speed = wave_speed[0]
    wetness = wet_mask[0].astype(jnp.float32)
    matrix = vertical[0]

    weights = intersection_weights[0, 0]
    pair_count, in_width, out_width = weights.shape
    tile_count = lax.axis_size("gx")
    grid_shape = surface_temp.shape[1:]
    cell_count = grid_shape[0] * grid_shape[1]
    in_blocks = cell_count // in_width
    out_blocks = cell_count // out_width
    sources = pair_source[0, 0]
    targets = pair_target[0, 0]
    target_tile = pair_tile[0, 0, :, 0]
    is_atmos = lax.axis_index("sec") == 0

    own_st = surface_temp[0].reshape(cell_count)
    own_wet = wetness.reshape(cell_count)
    drivers = jnp.stack(
        [model_state[0, 0, 0].reshape(cell_count), model_state[0, 1, 0].reshape(cell_count),
         model_state[0, 2, 0].reshape(cell_count), own_st]
    )
    zeros = jnp.zeros_like(own_st)
    sent = jnp.where(is_atmos, drivers, jnp.stack([own_st, own_wet, zeros, zeros]))
    got = lax.ppermute(sent, "sec", [(0, 1), (1, 0)])
    atmos_drivers = jnp.where(is_atmos, drivers, got)
    ocean_st = jnp.where(is_atmos, got[0], own_st)
    ocean_wet = jnp.where(is_atmos, got[1], own_wet)

    fluxes = jnp.tanh(jnp.dot(flux_coef, atmos_drivers, precision=HIGHEST_PRECISION)).astype(jnp.bfloat16)
    flux_count = fluxes.shape[0]
    blocks = fluxes.reshape(flux_count, in_blocks, in_width)
    picked = jnp.take(blocks, sources, axis=1)
    regridded = jnp.einsum(
        "fpi,pio->pfo", picked, weights, preferred_element_type=jnp.float32
    ).astype(jnp.bfloat16)
    heat = jnp.einsum(
        "f,pfo->po", heat_gain, regridded.astype(jnp.float32), precision=HIGHEST_PRECISION
    )

    capacity = max(2, 2 * pair_count // tile_count)
    slot_count = tile_count * capacity
    positions = jnp.arange(pair_count)
    same_tile = target_tile[None, :] == target_tile[:, None]
    is_before = positions[None, :] < positions[:, None]
    earlier = jnp.sum(same_tile & is_before, axis=1)
    slot_of = target_tile * capacity + earlier
    placing = jnp.arange(slot_count)[:, None] == slot_of[None, :]
    outgoing = jnp.dot(placing.astype(jnp.float32), heat, precision=HIGHEST_PRECISION)
    offsets = jnp.sum(jnp.where(placing, targets[None, :] + 1, 0), axis=1) - 1
    offset_row = jnp.zeros((tile_count, 1, out_width), jnp.float32).at[:, 0, :capacity].set(
        offsets.reshape(tile_count, capacity).astype(jnp.float32)
    )
    packet = jnp.concatenate([outgoing.reshape(tile_count, capacity, out_width), offset_row], axis=1)
    arrived = lax.all_to_all(packet, "gx", split_axis=0, concat_axis=0, tiled=True)
    arrived_at = arrived[:, capacity, :capacity].reshape(slot_count).astype(jnp.int32)
    landing = jnp.arange(out_blocks)[:, None] == arrived_at[None, :]
    heating = jnp.dot(
        landing.astype(jnp.float32),
        arrived[:, :capacity].reshape(slot_count, out_width),
        precision=HIGHEST_PRECISION,
    )
    ocean_temp = ocean_st + ocean_wet * heating.reshape(cell_count)

    returning = jnp.dot(
        landing.T.astype(jnp.bfloat16),
        ocean_temp.astype(jnp.bfloat16).reshape(out_blocks, out_width),
        preferred_element_type=jnp.float32,
    ).astype(jnp.bfloat16)
    delivered = lax.all_to_all(
        returning.reshape(tile_count, capacity, out_width), "gx", split_axis=0, concat_axis=0, tiled=True
    )
    carried = {}

    def tie(p2):
        carried["delivered"], p2 = lax.optimization_barrier((delivered, p2))
        return p2

    assert SUBSTEPS == 2
    p2, u2, v2 = stencil(pressure, eastward, northward, sound_speed, wetness, matrix, tie)
    final_state = jnp.stack([p2, u2, v2])[None]
    delivered = carried["delivered"]
    per_pair = jnp.dot(
        placing.T.astype(jnp.bfloat16),
        delivered.reshape(slot_count, out_width),
        preferred_element_type=jnp.float32,
    ).astype(jnp.bfloat16)
    pieces = jnp.einsum("pio,po->pi", weights, per_pair, preferred_element_type=jnp.float32)
    owning = (jnp.arange(in_blocks)[:, None] == sources[None, :]).astype(jnp.float32)
    atmos_temp = jnp.dot(owning, pieces, precision=HIGHEST_PRECISION)

    surface_temps = jnp.where(is_atmos, atmos_temp.reshape(grid_shape), ocean_temp.reshape(grid_shape))[None]
    return (final_state, surface_temps)


def solution(mesh):
    return jax.shard_map(
        local,
        mesh=mesh,
        in_specs=(
            P("sec", None, None, "gx", "gy"),
            P("sec", "gx", "gy"),
            P("sec", "gx", "gy"),
            P("sec", None, None),
            P("sec", "gx", "gy"),
            P(),
            P(),
            P("gx", "gy", None, None),
            P("gx", "gy", None),
            P("gx", "gy", None),
            P("gx", "gy", None, None, None),
        ),
        out_specs=(P("sec", None, None, "gx", "gy"), P("sec", "gx", "gy")),
        check_vma=False,
    )
```

```python
import jax
import jax.numpy as jnp
from jax import lax
from jax.sharding import PartitionSpec as P

SUBSTEPS = 2


HIGHEST_PRECISION = lax.Precision.HIGHEST


def neighbours(head, tail, axis):
    count = lax.axis_size(axis)
    me = lax.axis_index(axis)
    lo = lax.ppermute(tail, axis, [(i, (i + 1) % count) for i in range(count)])
    hi = lax.ppermute(head, axis, [((i + 1) % count, i) for i in range(count)])
    return jnp.where(me > 0, lo, 0.0), jnp.where(me < count - 1, hi, 0.0)


def vertical_mix(matrix, right_side):
    return right_side + jnp.einsum("lm,mxy->lxy", matrix, right_side, precision=HIGHEST_PRECISION)


def stencil(pressure, eastward, northward, sound_speed, wetness, matrix):
    wet3 = wetness[None]
    lo_x, hi_x = neighbours(
        jnp.concatenate([eastward[:, :1], wet3[:, :1]], axis=0),
        jnp.concatenate([eastward[:, -1:], wet3[:, -1:]], axis=0),
        "gx",
    )
    lo_y, hi_y = neighbours(
        jnp.concatenate([northward[:, :, :1], wet3[:, :, :1]], axis=0),
        jnp.concatenate([northward[:, :, -1:], wet3[:, :, -1:]], axis=0),
        "gy",
    )
    levels = eastward.shape[0]
    u_ext = jnp.concatenate([lo_x[:levels], eastward, hi_x[:levels]], axis=1)
    wet_x = jnp.concatenate([lo_x[levels:], wet3, hi_x[levels:]], axis=1)
    v_ext = jnp.concatenate([lo_y[:levels], northward, hi_y[:levels]], axis=2)
    wet_y = jnp.concatenate([lo_y[levels:], wet3, hi_y[levels:]], axis=2)

    divergence = (u_ext[:, 2:] - u_ext[:, :-2]) + (v_ext[:, :, 2:] - v_ext[:, :, :-2])
    p1 = vertical_mix(matrix, pressure - sound_speed * divergence)

    lo2x, hi2x = neighbours(p1[:, :2], p1[:, -2:], "gx")
    lo2y, hi2y = neighbours(p1[:, :, :2], p1[:, :, -2:], "gy")
    p1_x = jnp.concatenate([lo2x, p1, hi2x], axis=1)
    p1_y = jnp.concatenate([lo2y, p1, hi2y], axis=2)
    u1_ext = wet_x * (u_ext - 0.5 * (p1_x[:, 2:] - p1_x[:, :-2]))
    v1_ext = wet_y * (v_ext - 0.5 * (p1_y[:, :, 2:] - p1_y[:, :, :-2]))

    divergence = (u1_ext[:, 2:] - u1_ext[:, :-2]) + (v1_ext[:, :, 2:] - v1_ext[:, :, :-2])
    p2 = vertical_mix(matrix, p1 - sound_speed * divergence)

    lo3x, hi3x = neighbours(p2[:, :1], p2[:, -1:], "gx")
    lo3y, hi3y = neighbours(p2[:, :, :1], p2[:, :, -1:], "gy")
    p2_x = jnp.concatenate([lo3x, p2, hi3x], axis=1)
    p2_y = jnp.concatenate([lo3y, p2, hi3y], axis=2)
    u1 = u1_ext[:, 1:-1]
    v1 = v1_ext[:, :, 1:-1]
    u2 = wetness * (u1 - 0.5 * (p2_x[:, 2:] - p2_x[:, :-2]))
    v2 = wetness * (v1 - 0.5 * (p2_y[:, :, 2:] - p2_y[:, :, :-2]))
    return p2, u2, v2


def local(
    model_state,
    wave_speed,
    wet_mask,
    vertical,
    surface_temp,
    flux_coef,
    heat_gain,
    pair_tile,
    pair_source,
    pair_target,
    intersection_weights,
):
    pressure = model_state[0, 0]
    eastward = model_state[0, 1]
    northward = model_state[0, 2]
    sound_speed = wave_speed[0]
    wetness = wet_mask[0].astype(jnp.float32)
    matrix = vertical[0]
    assert SUBSTEPS == 2
    p2, u2, v2 = stencil(pressure, eastward, northward, sound_speed, wetness, matrix)
    final_state = jnp.stack([p2, u2, v2])[None]

    weights = intersection_weights[0, 0]
    pair_count, in_width, out_width = weights.shape
    tile_count = lax.axis_size("gx")
    grid_shape = surface_temp.shape[1:]
    cell_count = grid_shape[0] * grid_shape[1]
    in_blocks = cell_count // in_width
    out_blocks = cell_count // out_width
    sources = pair_source[0, 0]
    targets = pair_target[0, 0]
    target_tile = pair_tile[0, 0, :, 0]
    is_atmos = lax.axis_index("sec") == 0

    own_st = surface_temp[0].reshape(cell_count)
    own_wet = wetness.reshape(cell_count)
    drivers = jnp.stack(
        [model_state[0, 0, 0].reshape(cell_count), model_state[0, 1, 0].reshape(cell_count),
         model_state[0, 2, 0].reshape(cell_count), own_st]
    )
    zeros = jnp.zeros_like(own_st)
    sent = jnp.where(is_atmos, drivers, jnp.stack([own_st, own_wet, zeros, zeros]))
    got = lax.ppermute(sent, "sec", [(0, 1), (1, 0)])
    atmos_drivers = jnp.where(is_atmos, drivers, got)
    ocean_st = jnp.where(is_atmos, got[0], own_st)
    ocean_wet = jnp.where(is_atmos, got[1], own_wet)

    fluxes = jnp.tanh(jnp.dot(flux_coef, atmos_drivers, precision=HIGHEST_PRECISION)).astype(jnp.bfloat16)
    flux_count = fluxes.shape[0]
    blocks = fluxes.reshape(flux_count, in_blocks, in_width)
    picked = jnp.take(blocks, sources, axis=1)
    regridded = jnp.einsum(
        "fpi,pio->pfo", picked, weights, preferred_element_type=jnp.float32
    ).astype(jnp.bfloat16)
    heat = jnp.einsum(
        "f,pfo->po", heat_gain, regridded.astype(jnp.float32), precision=HIGHEST_PRECISION
    )

    capacity = max(2, 2 * pair_count // tile_count)
    slot_count = tile_count * capacity
    positions = jnp.arange(pair_count)
    same_tile = target_tile[None, :] == target_tile[:, None]
    is_before = positions[None, :] < positions[:, None]
    earlier = jnp.sum(same_tile & is_before, axis=1)
    slot_of = target_tile * capacity + earlier
    placing = jnp.arange(slot_count)[:, None] == slot_of[None, :]
    outgoing = jnp.dot(placing.astype(jnp.float32), heat, precision=HIGHEST_PRECISION)
    offsets = jnp.sum(jnp.where(placing, targets[None, :] + 1, 0), axis=1) - 1
    offset_row = jnp.zeros((tile_count, 1, out_width), jnp.float32).at[:, 0, :capacity].set(
        offsets.reshape(tile_count, capacity).astype(jnp.float32)
    )
    packet = jnp.concatenate([outgoing.reshape(tile_count, capacity, out_width), offset_row], axis=1)
    arrived = lax.all_to_all(packet, "gx", split_axis=0, concat_axis=0, tiled=True)
    arrived_at = arrived[:, capacity, :capacity].reshape(slot_count).astype(jnp.int32)
    landing = jnp.arange(out_blocks)[:, None] == arrived_at[None, :]
    heating = jnp.dot(
        landing.astype(jnp.float32),
        arrived[:, :capacity].reshape(slot_count, out_width),
        precision=HIGHEST_PRECISION,
    )
    ocean_temp = ocean_st + ocean_wet * heating.reshape(cell_count)

    returning = jnp.dot(
        landing.T.astype(jnp.bfloat16),
        ocean_temp.astype(jnp.bfloat16).reshape(out_blocks, out_width),
        preferred_element_type=jnp.float32,
    ).astype(jnp.bfloat16)
    delivered = lax.all_to_all(
        returning.reshape(tile_count, capacity, out_width), "gx", split_axis=0, concat_axis=0, tiled=True
    )
    per_pair = jnp.dot(
        placing.T.astype(jnp.bfloat16),
        delivered.reshape(slot_count, out_width),
        preferred_element_type=jnp.float32,
    ).astype(jnp.bfloat16)
    pieces = jnp.einsum("pio,po->pi", weights, per_pair, preferred_element_type=jnp.float32)
    owning = (jnp.arange(in_blocks)[:, None] == sources[None, :]).astype(jnp.float32)
    atmos_temp = jnp.dot(owning, pieces, precision=HIGHEST_PRECISION)

    surface_temps = jnp.where(is_atmos, atmos_temp.reshape(grid_shape), ocean_temp.reshape(grid_shape))[None]
    return (final_state, surface_temps)


def solution(mesh):
    return jax.shard_map(
        local,
        mesh=mesh,
        in_specs=(
            P("sec", None, None, "gx", "gy"),
            P("sec", "gx", "gy"),
            P("sec", "gx", "gy"),
            P("sec", None, None),
            P("sec", "gx", "gy"),
            P(),
            P(),
            P("gx", "gy", None, None),
            P("gx", "gy", None),
            P("gx", "gy", None),
            P("gx", "gy", None, None, None),
        ),
        out_specs=(P("sec", None, None, "gx", "gy"), P("sec", "gx", "gy")),
        check_vma=False,
    )
```

```python
import jax
import jax.numpy as jnp
from jax import lax
from jax.sharding import PartitionSpec as P

SUBSTEPS = 2


HIGHEST_PRECISION = lax.Precision.HIGHEST


def neighbours(head, tail, axis):
    count = lax.axis_size(axis)
    me = lax.axis_index(axis)
    tail = jnp.where(me < count - 1, tail, 0.0)
    head = jnp.where(me > 0, head, 0.0)
    lo = lax.ppermute(tail, axis, [(i, (i + 1) % count) for i in range(count)])
    hi = lax.ppermute(head, axis, [((i + 1) % count, i) for i in range(count)])
    return lo, hi


def vertical_mix(matrix, right_side):
    return right_side + jnp.einsum("lm,mxy->lxy", matrix, right_side, precision=HIGHEST_PRECISION)


def stencil(pressure, eastward, northward, sound_speed, wetness, matrix):
    wet3 = wetness[None]
    lo_x, hi_x = neighbours(
        jnp.concatenate([eastward[:, :1], wet3[:, :1]], axis=0),
        jnp.concatenate([eastward[:, -1:], wet3[:, -1:]], axis=0),
        "gx",
    )
    lo_y, hi_y = neighbours(
        jnp.concatenate([northward[:, :, :1], wet3[:, :, :1]], axis=0),
        jnp.concatenate([northward[:, :, -1:], wet3[:, :, -1:]], axis=0),
        "gy",
    )
    levels = eastward.shape[0]
    u_ext = jnp.concatenate([lo_x[:levels], eastward, hi_x[:levels]], axis=1)
    wet_x = jnp.concatenate([lo_x[levels:], wet3, hi_x[levels:]], axis=1)
    v_ext = jnp.concatenate([lo_y[:levels], northward, hi_y[:levels]], axis=2)
    wet_y = jnp.concatenate([lo_y[levels:], wet3, hi_y[levels:]], axis=2)

    divergence = (u_ext[:, 2:] - u_ext[:, :-2]) + (v_ext[:, :, 2:] - v_ext[:, :, :-2])
    p1 = vertical_mix(matrix, pressure - sound_speed * divergence)

    lo2x, hi2x = neighbours(p1[:, :2], p1[:, -2:], "gx")
    lo2y, hi2y = neighbours(p1[:, :, :2], p1[:, :, -2:], "gy")
    p1_x = jnp.concatenate([lo2x, p1, hi2x], axis=1)
    p1_y = jnp.concatenate([lo2y, p1, hi2y], axis=2)
    u1_ext = wet_x * (u_ext - 0.5 * (p1_x[:, 2:] - p1_x[:, :-2]))
    v1_ext = wet_y * (v_ext - 0.5 * (p1_y[:, :, 2:] - p1_y[:, :, :-2]))

    divergence = (u1_ext[:, 2:] - u1_ext[:, :-2]) + (v1_ext[:, :, 2:] - v1_ext[:, :, :-2])
    p2 = vertical_mix(matrix, p1 - sound_speed * divergence)

    lo3x, hi3x = neighbours(p2[:, :1], p2[:, -1:], "gx")
    lo3y, hi3y = neighbours(p2[:, :, :1], p2[:, :, -1:], "gy")
    p2_x = jnp.concatenate([lo3x, p2, hi3x], axis=1)
    p2_y = jnp.concatenate([lo3y, p2, hi3y], axis=2)
    u1 = u1_ext[:, 1:-1]
    v1 = v1_ext[:, :, 1:-1]
    u2 = wetness * (u1 - 0.5 * (p2_x[:, 2:] - p2_x[:, :-2]))
    v2 = wetness * (v1 - 0.5 * (p2_y[:, :, 2:] - p2_y[:, :, :-2]))
    return p2, u2, v2


def local(
    model_state,
    wave_speed,
    wet_mask,
    vertical,
    surface_temp,
    flux_coef,
    heat_gain,
    pair_tile,
    pair_source,
    pair_target,
    intersection_weights,
):
    pressure = model_state[0, 0]
    eastward = model_state[0, 1]
    northward = model_state[0, 2]
    sound_speed = wave_speed[0]
    wetness = wet_mask[0].astype(jnp.float32)
    matrix = vertical[0]
    assert SUBSTEPS == 2
    p2, u2, v2 = stencil(pressure, eastward, northward, sound_speed, wetness, matrix)
    final_state = jnp.stack([p2, u2, v2])[None]

    weights = intersection_weights[0, 0]
    pair_count, in_width, out_width = weights.shape
    tile_count = lax.axis_size("gx")
    grid_shape = surface_temp.shape[1:]
    cell_count = grid_shape[0] * grid_shape[1]
    in_blocks = cell_count // in_width
    out_blocks = cell_count // out_width
    sources = pair_source[0, 0]
    targets = pair_target[0, 0]
    target_tile = pair_tile[0, 0, :, 0]
    is_atmos = lax.axis_index("sec") == 0

    own_st = surface_temp[0].reshape(cell_count)
    own_wet = wetness.reshape(cell_count)
    drivers = jnp.stack(
        [model_state[0, 0, 0].reshape(cell_count), model_state[0, 1, 0].reshape(cell_count),
         model_state[0, 2, 0].reshape(cell_count), own_st]
    )
    zeros = jnp.zeros_like(own_st)
    sent = jnp.where(is_atmos, drivers, jnp.stack([own_st, own_wet, zeros, zeros]))
    got = lax.ppermute(sent, "sec", [(0, 1), (1, 0)])
    atmos_drivers = jnp.where(is_atmos, drivers, got)
    ocean_st = jnp.where(is_atmos, got[0], own_st)
    ocean_wet = jnp.where(is_atmos, got[1], own_wet)

    fluxes = jnp.tanh(jnp.dot(flux_coef, atmos_drivers, precision=HIGHEST_PRECISION)).astype(jnp.bfloat16)
    flux_count = fluxes.shape[0]
    blocks = fluxes.reshape(flux_count, in_blocks, in_width)
    picked = jnp.take(blocks, sources, axis=1)
    regridded = jnp.einsum(
        "fpi,pio->pfo", picked, weights, preferred_element_type=jnp.float32
    ).astype(jnp.bfloat16)
    heat = jnp.einsum(
        "f,pfo->po", heat_gain, regridded.astype(jnp.float32), precision=HIGHEST_PRECISION
    )

    capacity = max(2, 2 * pair_count // tile_count)
    slot_count = tile_count * capacity
    positions = jnp.arange(pair_count)
    same_tile = target_tile[None, :] == target_tile[:, None]
    is_before = positions[None, :] < positions[:, None]
    earlier = jnp.sum(same_tile & is_before, axis=1)
    slot_of = target_tile * capacity + earlier
    placing = jnp.arange(slot_count)[:, None] == slot_of[None, :]
    outgoing = jnp.dot(placing.astype(jnp.float32), heat, precision=HIGHEST_PRECISION)
    offsets = jnp.sum(jnp.where(placing, targets[None, :] + 1, 0), axis=1) - 1
    offset_row = jnp.zeros((tile_count, 1, out_width), jnp.float32).at[:, 0, :capacity].set(
        offsets.reshape(tile_count, capacity).astype(jnp.float32)
    )
    packet = jnp.concatenate([outgoing.reshape(tile_count, capacity, out_width), offset_row], axis=1)
    arrived = lax.all_to_all(packet, "gx", split_axis=0, concat_axis=0, tiled=True)
    arrived_at = arrived[:, capacity, :capacity].reshape(slot_count).astype(jnp.int32)
    landing = jnp.arange(out_blocks)[:, None] == arrived_at[None, :]
    heating = jnp.dot(
        landing.astype(jnp.float32),
        arrived[:, :capacity].reshape(slot_count, out_width),
        precision=HIGHEST_PRECISION,
    )
    ocean_temp = ocean_st + ocean_wet * heating.reshape(cell_count)

    returning = jnp.dot(
        landing.T.astype(jnp.bfloat16),
        ocean_temp.astype(jnp.bfloat16).reshape(out_blocks, out_width),
        preferred_element_type=jnp.float32,
    ).astype(jnp.bfloat16)
    delivered = lax.all_to_all(
        returning.reshape(tile_count, capacity, out_width), "gx", split_axis=0, concat_axis=0, tiled=True
    )
    per_pair = jnp.dot(
        placing.T.astype(jnp.bfloat16),
        delivered.reshape(slot_count, out_width),
        preferred_element_type=jnp.float32,
    ).astype(jnp.bfloat16)
    pieces = jnp.einsum("pio,po->pi", weights, per_pair, preferred_element_type=jnp.float32)
    owning = (jnp.arange(in_blocks)[:, None] == sources[None, :]).astype(jnp.float32)
    atmos_temp = jnp.dot(owning, pieces, precision=HIGHEST_PRECISION)

    surface_temps = jnp.where(is_atmos, atmos_temp.reshape(grid_shape), ocean_temp.reshape(grid_shape))[None]
    return (final_state, surface_temps)


def solution(mesh):
    return jax.shard_map(
        local,
        mesh=mesh,
        in_specs=(
            P("sec", None, None, "gx", "gy"),
            P("sec", "gx", "gy"),
            P("sec", "gx", "gy"),
            P("sec", None, None),
            P("sec", "gx", "gy"),
            P(),
            P(),
            P("gx", "gy", None, None),
            P("gx", "gy", None),
            P("gx", "gy", None),
            P("gx", "gy", None, None, None),
        ),
        out_specs=(P("sec", None, None, "gx", "gy"), P("sec", "gx", "gy")),
        check_vma=False,
    )
```

```python
import jax
import jax.numpy as jnp
from jax import lax
from jax.sharding import PartitionSpec as P

SUBSTEPS = 2


HIGHEST_PRECISION = lax.Precision.HIGHEST


def neighbours(head, tail, axis):
    count = lax.axis_size(axis)
    me = lax.axis_index(axis)
    tail = jnp.where(me < count - 1, tail, 0.0)
    head = jnp.where(me > 0, head, 0.0)
    lo = lax.ppermute(tail, axis, [(i, (i + 1) % count) for i in range(count)])
    hi = lax.ppermute(head, axis, [((i + 1) % count, i) for i in range(count)])
    return lo, hi


def vertical_mix(matrix, right_side):
    return right_side + jnp.einsum("lm,mxy->lxy", matrix, right_side, precision=HIGHEST_PRECISION)


def stencil(pressure, eastward, northward, sound_speed, wetness, matrix):
    wet3 = wetness[None]
    lo_x, hi_x = neighbours(
        jnp.concatenate([eastward[:, :1], wet3[:, :1]], axis=0),
        jnp.concatenate([eastward[:, -1:], wet3[:, -1:]], axis=0),
        "gx",
    )
    lo_y, hi_y = neighbours(
        jnp.concatenate([northward[:, :, :1], wet3[:, :, :1]], axis=0),
        jnp.concatenate([northward[:, :, -1:], wet3[:, :, -1:]], axis=0),
        "gy",
    )
    levels = eastward.shape[0]
    u_ext = jnp.concatenate([lo_x[:levels], eastward, hi_x[:levels]], axis=1)
    wet_x = jnp.concatenate([lo_x[levels:], wet3, hi_x[levels:]], axis=1)
    v_ext = jnp.concatenate([lo_y[:levels], northward, hi_y[:levels]], axis=2)
    wet_y = jnp.concatenate([lo_y[levels:], wet3, hi_y[levels:]], axis=2)

    divergence = (u_ext[:, 2:] - u_ext[:, :-2]) + (v_ext[:, :, 2:] - v_ext[:, :, :-2])
    p1 = vertical_mix(matrix, pressure - sound_speed * divergence)

    lo2x, hi2x = neighbours(p1[:, :2], p1[:, -2:], "gx")
    lo2y, hi2y = neighbours(p1[:, :, :2], p1[:, :, -2:], "gy")
    p1_x = jnp.concatenate([lo2x, p1, hi2x], axis=1)
    p1_y = jnp.concatenate([lo2y, p1, hi2y], axis=2)
    u1_ext = wet_x * (u_ext - 0.5 * (p1_x[:, 2:] - p1_x[:, :-2]))
    v1_ext = wet_y * (v_ext - 0.5 * (p1_y[:, :, 2:] - p1_y[:, :, :-2]))

    divergence = (u1_ext[:, 2:] - u1_ext[:, :-2]) + (v1_ext[:, :, 2:] - v1_ext[:, :, :-2])
    p2 = vertical_mix(matrix, p1 - sound_speed * divergence)

    lo3x, hi3x = neighbours(p2[:, :1], p2[:, -1:], "gx")
    lo3y, hi3y = neighbours(p2[:, :, :1], p2[:, :, -1:], "gy")
    p2_x = jnp.concatenate([lo3x, p2, hi3x], axis=1)
    p2_y = jnp.concatenate([lo3y, p2, hi3y], axis=2)
    u1 = u1_ext[:, 1:-1]
    v1 = v1_ext[:, :, 1:-1]
    u2 = wetness * (u1 - 0.5 * (p2_x[:, 2:] - p2_x[:, :-2]))
    v2 = wetness * (v1 - 0.5 * (p2_y[:, :, 2:] - p2_y[:, :, :-2]))
    return p2, u2, v2


def local(
    model_state,
    wave_speed,
    wet_mask,
    vertical,
    surface_temp,
    flux_coef,
    heat_gain,
    pair_tile,
    pair_source,
    pair_target,
    intersection_weights,
):
    pressure = model_state[0, 0]
    eastward = model_state[0, 1]
    northward = model_state[0, 2]
    sound_speed = wave_speed[0]
    wetness = wet_mask[0].astype(jnp.float32)
    matrix = vertical[0]
    assert SUBSTEPS == 2
    p2, u2, v2 = stencil(pressure, eastward, northward, sound_speed, wetness, matrix)
    final_state = jnp.stack([p2, u2, v2])[None]

    weights = intersection_weights[0, 0]
    pair_count, in_width, out_width = weights.shape
    tile_count = lax.axis_size("gx")
    grid_shape = surface_temp.shape[1:]
    cell_count = grid_shape[0] * grid_shape[1]
    in_blocks = cell_count // in_width
    out_blocks = cell_count // out_width
    sources = pair_source[0, 0]
    targets = pair_target[0, 0]
    target_tile = pair_tile[0, 0, :, 0]
    is_atmos = lax.axis_index("sec") == 0

    own_st = surface_temp[0].reshape(cell_count)
    own_wet = wetness.reshape(cell_count)
    drivers = jnp.stack(
        [model_state[0, 0, 0].reshape(cell_count), model_state[0, 1, 0].reshape(cell_count),
         model_state[0, 2, 0].reshape(cell_count), own_st]
    )
    got = lax.ppermute(jnp.concatenate([drivers, own_wet[None]]), "sec", [(0, 1), (1, 0)])
    atmos_drivers = jnp.where(is_atmos, drivers, got[:4])
    ocean_st = jnp.where(is_atmos, got[3], own_st)
    ocean_wet = jnp.where(is_atmos, got[4], own_wet)

    fluxes = jnp.tanh(jnp.dot(flux_coef, atmos_drivers, precision=HIGHEST_PRECISION)).astype(jnp.bfloat16)
    flux_count = fluxes.shape[0]
    blocks = fluxes.reshape(flux_count, in_blocks, in_width)
    picked = jnp.take(blocks, sources, axis=1)
    regridded = jnp.einsum(
        "fpi,pio->pfo", picked, weights, preferred_element_type=jnp.float32
    ).astype(jnp.bfloat16)
    heat = jnp.einsum(
        "f,pfo->po", heat_gain, regridded.astype(jnp.float32), precision=HIGHEST_PRECISION
    )

    capacity = max(2, 2 * pair_count // tile_count)
    slot_count = tile_count * capacity
    positions = jnp.arange(pair_count)
    same_tile = target_tile[None, :] == target_tile[:, None]
    is_before = positions[None, :] < positions[:, None]
    earlier = jnp.sum(same_tile & is_before, axis=1)
    slot_of = target_tile * capacity + earlier
    placing = jnp.arange(slot_count)[:, None] == slot_of[None, :]
    outgoing = jnp.dot(placing.astype(jnp.float32), heat, precision=HIGHEST_PRECISION)
    offsets = jnp.sum(jnp.where(placing, targets[None, :] + 1, 0), axis=1) - 1
    offset_row = jnp.zeros((tile_count, 1, out_width), jnp.float32).at[:, 0, :capacity].set(
        offsets.reshape(tile_count, capacity).astype(jnp.float32)
    )
    packet = jnp.concatenate([outgoing.reshape(tile_count, capacity, out_width), offset_row], axis=1)
    arrived = lax.all_to_all(packet, "gx", split_axis=0, concat_axis=0, tiled=True)
    arrived_at = arrived[:, capacity, :capacity].reshape(slot_count).astype(jnp.int32)
    landing = jnp.arange(out_blocks)[:, None] == arrived_at[None, :]
    heating = jnp.dot(
        landing.astype(jnp.float32),
        arrived[:, :capacity].reshape(slot_count, out_width),
        precision=HIGHEST_PRECISION,
    )
    ocean_temp = ocean_st + ocean_wet * heating.reshape(cell_count)

    returning = jnp.dot(
        landing.T.astype(jnp.bfloat16),
        ocean_temp.astype(jnp.bfloat16).reshape(out_blocks, out_width),
        preferred_element_type=jnp.float32,
    ).astype(jnp.bfloat16)
    delivered = lax.all_to_all(
        returning.reshape(tile_count, capacity, out_width), "gx", split_axis=0, concat_axis=0, tiled=True
    )
    per_pair = jnp.dot(
        placing.T.astype(jnp.bfloat16),
        delivered.reshape(slot_count, out_width),
        preferred_element_type=jnp.float32,
    ).astype(jnp.bfloat16)
    pieces = jnp.einsum("pio,po->pi", weights, per_pair, preferred_element_type=jnp.float32)
    owning = (jnp.arange(in_blocks)[:, None] == sources[None, :]).astype(jnp.float32)
    atmos_temp = jnp.dot(owning, pieces, precision=HIGHEST_PRECISION)

    surface_temps = jnp.where(is_atmos, atmos_temp.reshape(grid_shape), ocean_temp.reshape(grid_shape))[None]
    return (final_state, surface_temps)


def solution(mesh):
    return jax.shard_map(
        local,
        mesh=mesh,
        in_specs=(
            P("sec", None, None, "gx", "gy"),
            P("sec", "gx", "gy"),
            P("sec", "gx", "gy"),
            P("sec", None, None),
            P("sec", "gx", "gy"),
            P(),
            P(),
            P("gx", "gy", None, None),
            P("gx", "gy", None),
            P("gx", "gy", None),
            P("gx", "gy", None, None, None),
        ),
        out_specs=(P("sec", None, None, "gx", "gy"), P("sec", "gx", "gy")),
        check_vma=False,
    )
```
